32 devices in a mesh: groups: 2 (over y), ctx: 4 (over z), head: 4 (over x, core).
Axes of the slice: x: 2, y: 2, z: 4, core: 2. Of those that a mesh axis runs over, the one named last changes fastest.
Arguments:
- q_block: bfloat16 [2048, 8192], P(('groups', 'ctx'), 'head'), parts along dimension 0, may hold values from -6 to 6
- kv_block: bfloat16 [2, 2048, 1024], P(None, ('groups', 'ctx'), 'head'), parts along dimension 1, may hold values from -6 to 6
- anchor_kv: bfloat16 [2, 1024, 1024], P(None, ('groups', 'ctx'), 'head'), parts along dimension 1, may hold values from -6 to 6
- cache_kv: bfloat16 [2, 32768, 1024], P(None, ('groups', 'ctx'), 'head'), parts along dimension 1, may hold values from -6 to 6
- cache_len: int32 [8], P(('groups', 'ctx')), parts along dimension 0, may hold values from 1 to 4096, 8192 in all
- query_q: bfloat16 [128, 8192], P(('groups', 'ctx'), 'head'), parts along dimension 0, may hold values from -6 to 6
- query_kv: bfloat16 [2, 128, 1024], P(None, ('groups', 'ctx'), 'head'), parts along dimension 1, may hold values from -6 to 6
- query_pos: int32 [128], P('groups'), parts along dimension 0, may hold values from 0 to 63, each once
Outputs:
- block_out: bfloat16 [2048, 8192], P(('groups', 'ctx'), 'head'), parts along dimension 0
- query_out: bfloat16 [128, 8192], P(('groups', 'ctx'), 'head'), parts along dimension 0
The draws below stay inside these ranges and needn't reach their ends.
There are 2 independent parts, one for each index of `groups`. The reference program is written for one: setup_inputs(seed, part) draws one part's arguments, and reference() takes and returns one part's arrays. A program takes and returns all parts, laid end to end along the dimension named above; each array names one. Nothing has to cross between parts.
All inputs are finite; a program needn't handle non-finite values. No bound on the sum of `cache_len` on one device may be relied on, other than what follows from the above.
Results may differ from the reference program's by a relative error of at most 0.0034.
Values may be sent and summed in bfloat16 or wider, within the bound.
No kernel may reach another device: no remote copies, remote signals or barrier semaphores. Data moves between devices by JAX's collectives and lax.ppermute only.
A program may use at most 128 MiB of HBM per device.

```python
import math
import jax
import jax.numpy as jnp
import numpy as np
from jax import lax

HQ = 64
KVH = 8
HD = 128
CACHE_DEV = 4096
BLK = 256
ANCHOR = 512
QTOK = 64
HOSTS = 4


def pair_rows(key, salt, row_total, span):
    own_key = jax.random.fold_in(key, salt)
    noise = jax.random.normal(jax.random.fold_in(own_key, 1), (2, row_total, KVH * HD), jnp.float32)
    centers = jax.random.normal(jax.random.fold_in(own_key, 2), (2, row_total // span, KVH * HD), jnp.float32)
    centers = jnp.repeat(centers, span, axis=1)
    key_part = noise[0] + 0.8 * centers[0]
    value_part = 0.6 * noise[1] + centers[1]
    return jnp.clip(jnp.stack([key_part, value_part]), -6.0, 6.0).astype(jnp.bfloat16)


def query_rows(key, salt, row_total):
    base = jax.random.normal(jax.random.fold_in(key, salt), (row_total, HQ * HD), jnp.float32)
    base = jnp.clip(base, -6.0, 6.0)
    return base.astype(jnp.bfloat16)


def draw_q_block(key, part):
    return query_rows(key, 11, HOSTS * BLK)


def draw_anchor_kv(key, part):
    return pair_rows(key, 12, ANCHOR, 2)


def draw_kv_block(key, part):
    return pair_rows(key, 13, HOSTS * BLK, BLK)


def draw_cache_kv(key, part):
    return pair_rows(key, 14, HOSTS * CACHE_DEV, CACHE_DEV)


def draw_query_q(key, part):
    return query_rows(key, 15, QTOK)


def draw_query_kv(key, part):
    return pair_rows(key, 16, QTOK, 2)


def length_profile(count, total, most, slope):
    weights = [(1 << 20) // math.isqrt(rank ** slope) + 1 for rank in range(2, count + 1)]
    spare, holding = total - most - (count - 1), [1] * (count - 1)
    while spare > 0:
        free = [i for i in range(count - 1) if holding[i] < most]
        mass, budget = sum([weights[i] for i in free]), spare
        for i in free:
            extra = min(most - holding[i], max(1, budget * weights[i] // mass), spare)
            holding[i] = holding[i] + extra
            spare = spare - extra
    return np.array([most] + holding)


def ragged(key, number_of, total, most, slope):
    if number_of == 2:
        one = jax.random.randint(key, (), max(1, total - most), min(most, total - 1) + 1)
        return jnp.stack([one, total - one])
    tallies = jnp.asarray(length_profile(number_of, total, most, slope), jnp.int32)
    twos = (number_of - 1) // 2
    donor, taker = tallies[1:1 + 2 * twos:2], tallies[2:2 + 2 * twos:2]
    room = jnp.minimum(donor - 1, most - taker)
    moved = jax.random.randint(jax.random.fold_in(key, 1), (twos,), 0, 1 << 20) % (room + 1)
    tallies = tallies.at[1:1 + 2 * twos:2].set(donor - moved).at[2:2 + 2 * twos:2].set(taker + moved)
    return tallies[jax.random.permutation(jax.random.fold_in(key, 2), number_of)]


def setup_inputs(seed: int = 0, part: int = 0) -> dict:
    key_of = jax.random.split(jax.random.key(seed), 9)
    part_splits = jax.random.split(jax.random.fold_in(key_of[8], part), 9)
    return {
        "q_block": draw_q_block(jax.random.fold_in(jax.random.fold_in(key_of[8], part), 71), part),
        "kv_block": draw_kv_block(jax.random.fold_in(jax.random.fold_in(key_of[8], part), 71), part),
        "anchor_kv": draw_anchor_kv(jax.random.fold_in(jax.random.fold_in(key_of[8], part), 71), part),
        "cache_kv": draw_cache_kv(jax.random.fold_in(jax.random.fold_in(key_of[8], part), 71), part),
        "cache_len": ragged(part_splits[4], HOSTS, HOSTS * CACHE_DEV // 2, CACHE_DEV, 2).astype(jnp.int32),
        "query_q": draw_query_q(jax.random.fold_in(jax.random.fold_in(key_of[8], part), 71), part),
        "query_kv": draw_query_kv(jax.random.fold_in(jax.random.fold_in(key_of[8], part), 71), part),
        "query_pos": jax.random.permutation(part_splits[7], QTOK).astype(jnp.int32),
    }


masked_score = -1e+30

def widen(per_head):
    return jnp.repeat(per_head, HD, axis=-1)

def partial_attention(queries, key_rows, value_rows, visible):
    row_count = queries.shape[0]
    key_count = key_rows.shape[0]
    kv_heads = key_rows.shape[1] // HD
    query_heads = queries.shape[1] // HD
    group_size = query_heads // kv_heads
    grouped = queries.astype(jnp.float32).reshape(row_count, kv_heads, group_size, HD)
    key_heads = key_rows.astype(jnp.float32).reshape(key_count, kv_heads, HD)
    scores = jnp.einsum('rkgd,skd->rkgs', grouped, key_heads, precision=lax.Precision.HIGHEST) * (1.0 / jnp.sqrt(jnp.float32(HD)))
    scores = jnp.where(visible[:, None, None, :], scores, masked_score)
    peak_score = lax.optimization_barrier(jnp.max(scores, axis=-1))
    weights = jnp.exp(scores - peak_score[..., None])
    totals = lax.optimization_barrier(jnp.sum(weights, axis=-1))
    rounded = weights.astype(jnp.bfloat16).astype(jnp.float32)
    value_heads = value_rows.astype(jnp.float32).reshape(key_count, kv_heads, HD)
    output = jnp.einsum('rkgs,skd->rkgd', rounded, value_heads, precision=lax.Precision.HIGHEST)
    return (peak_score.reshape(row_count, query_heads), totals.reshape(row_count, query_heads), output.reshape(row_count, query_heads * HD))

def reference(q_block, kv_block, anchor_kv, cache_kv, cache_len, query_q, query_kv, query_pos):
    causal = jnp.arange(BLK)[None, :] <= jnp.arange(BLK)[:, None]
    block_visible = jnp.concatenate([jnp.ones((BLK, ANCHOR), bool), causal], axis=1)

    def encode(host_index):
        block_rows = lax.dynamic_slice_in_dim(q_block, host_index * BLK, BLK, 0)
        block_pair = lax.dynamic_slice_in_dim(kv_block, host_index * BLK, BLK, 1)
        parts = partial_attention(block_rows, jnp.concatenate([anchor_kv[0], block_pair[0]], axis=0), jnp.concatenate([anchor_kv[1], block_pair[1]], axis=0), block_visible)
        return (parts[2] / widen(parts[1])).astype(jnp.bfloat16)
    block_out = lax.map(encode, jnp.arange(HOSTS, dtype=jnp.int32)).reshape(HOSTS * BLK, HQ * HD)

    def context(host_index):
        cache_pair = lax.dynamic_slice_in_dim(cache_kv, host_index * CACHE_DEV, CACHE_DEV, 1)
        block_pair = lax.dynamic_slice_in_dim(kv_block, host_index * BLK, BLK, 1)
        in_cache = jnp.arange(CACHE_DEV, dtype=jnp.int32) < cache_len[host_index]
        visible = jnp.concatenate([jnp.broadcast_to(in_cache[None, :], (QTOK, CACHE_DEV)), jnp.ones((QTOK, BLK), bool)], axis=1)
        return partial_attention(query_q, jnp.concatenate([cache_pair[0], block_pair[0]], axis=0), jnp.concatenate([cache_pair[1], block_pair[1]], axis=0), visible)
    peaks, totals, outputs = lax.map(context, jnp.arange(HOSTS, dtype=jnp.int32))
    local_visible = jnp.concatenate([jnp.ones((QTOK, ANCHOR), bool), query_pos[None, :] <= query_pos[:, None]], axis=1)
    local_peak, local_totals, local_output = partial_attention(query_q, jnp.concatenate([anchor_kv[0], query_kv[0]], axis=0), jnp.concatenate([anchor_kv[1], query_kv[1]], axis=0), local_visible)
    top_score = jnp.maximum(lax.optimization_barrier(jnp.max(peaks, axis=0)), local_peak)
    factors = jnp.exp(peaks - top_score[None])
    local_factor = jnp.exp(local_peak - top_score)
    merged_totals = lax.optimization_barrier(jnp.sum(totals * factors, axis=0)) + local_totals * local_factor
    merged_output = lax.optimization_barrier(jnp.sum(outputs * widen(factors), axis=0)) + local_output * widen(local_factor)
    return (block_out, (merged_output / widen(merged_totals)).astype(jnp.bfloat16))
```

```python
import jax
import jax.numpy as jnp
from jax import lax
from jax.sharding import PartitionSpec as P

HD = 128


masked_score = -1e30


def widen(per_head):
    return jnp.repeat(per_head, HD, axis=-1)


def partial_attention(queries, parts):
    row_count = queries.shape[0]
    kv_heads = parts[0][0].shape[1] // HD
    query_heads = queries.shape[1] // HD
    group_size = query_heads // kv_heads
    grouped = queries.reshape(row_count, kv_heads, group_size, HD)
    scale = 1.0 / jnp.sqrt(jnp.float32(HD))
    all_scores = []
    for key_rows, _, visible in parts:
        key_heads = key_rows.reshape(key_rows.shape[0], kv_heads, HD)
        scores = jnp.einsum(
            "rkgd,skd->rkgs", grouped, key_heads, preferred_element_type=jnp.float32
        ) * scale
        if visible is not None:
            scores = jnp.where(visible[:, None, None, :], scores, masked_score)
        all_scores.append(scores)
    peak_score = all_scores[0].max(axis=-1)
    for scores in all_scores[1:]:
        peak_score = jnp.maximum(peak_score, scores.max(axis=-1))
    totals = None
    output = None
    for scores, (_, value_rows, _) in zip(all_scores, parts):
        weights = jnp.exp(scores - peak_score[..., None])
        part_total = jnp.sum(weights, axis=-1)
        value_heads = value_rows.reshape(value_rows.shape[0], kv_heads, HD)
        part_output = jnp.einsum(
            "rkgs,skd->rkgd",
            weights.astype(jnp.bfloat16),
            value_heads,
            preferred_element_type=jnp.float32,
        )
        totals = part_total if totals is None else totals + part_total
        output = part_output if output is None else output + part_output
    return (
        peak_score.reshape(row_count, query_heads),
        totals.reshape(row_count, query_heads),
        output.reshape(row_count, query_heads * HD),
    )


def shifted(value, shift, count):
    return lax.ppermute(value, "ctx", [(j, (j + shift) % count) for j in range(count)])


def make_local(ctx_count):
    def local(q_block, kv_block, anchor_kv, cache_kv, cache_len, query_q, query_kv, query_pos):
        me = lax.axis_index("ctx")
        own_count = query_q.shape[0]
        anchor_rows = anchor_kv.shape[1]
        width = kv_block.shape[2]
        pieces = (anchor_kv.reshape(-1), query_q.reshape(-1), query_kv.reshape(-1))
        sizes = [piece.shape[0] for piece in pieces]
        packed = jnp.concatenate(pieces)
        slots = [packed] + [shifted(packed, k, ctx_count) for k in range(1, ctx_count)]

        def unpack(slot):
            a = slot[: sizes[0]].reshape(2, anchor_rows, width)
            q = slot[sizes[0] : sizes[0] + sizes[1]].reshape(own_count, -1)
            kv = slot[sizes[0] + sizes[1] :].reshape(2, own_count, width)
            return a, q, kv

        unpacked = [unpack(slot) for slot in slots]
        anchor = jnp.concatenate([u[0] for u in unpacked], axis=1)
        all_queries = jnp.concatenate([u[1] for u in unpacked], axis=0)
        all_query_kv = jnp.concatenate([u[2] for u in unpacked], axis=1)
        slot_pos = jnp.concatenate(
            [
                lax.dynamic_slice_in_dim(query_pos, ((me - k) % ctx_count) * own_count, own_count)
                for k in range(ctx_count)
            ]
        )
        own_pos = slot_pos[:own_count]

        block_count = q_block.shape[0]
        causal = jnp.arange(block_count)[None, :] <= jnp.arange(block_count)[:, None]
        block_parts = partial_attention(
            q_block,
            [(anchor[0], anchor[1], None), (kv_block[0], kv_block[1], causal)],
        )
        block_out = (block_parts[2] / widen(block_parts[1])).astype(jnp.bfloat16)

        cache_count = cache_kv.shape[1]
        in_cache = (jnp.arange(cache_count, dtype=jnp.int32) < cache_len[0])[None, :]
        context_peak, context_totals, context_output = partial_attention(
            all_queries,
            [(cache_kv[0], cache_kv[1], in_cache), (kv_block[0], kv_block[1], None)],
        )
        local_parts = partial_attention(
            query_q,
            [
                (anchor[0], anchor[1], None),
                (all_query_kv[0], all_query_kv[1], slot_pos[None, :] <= own_pos[:, None]),
            ],
        )
        heads = context_peak.shape[1]
        context_packed = jnp.concatenate([context_output, context_peak, context_totals], axis=1)
        remote = [context_packed[:own_count]]
        for k in range(1, ctx_count):
            section = context_packed[k * own_count : (k + 1) * own_count]
            remote.append(shifted(section, -k, ctx_count))
        peaks = [local_parts[0]] + [r[:, -2 * heads : -heads] for r in remote]
        totals = [local_parts[1]] + [r[:, -heads:] for r in remote]
        outputs = [local_parts[2]] + [r[:, : -2 * heads] for r in remote]
        top_score = peaks[0]
        for peak in peaks[1:]:
            top_score = jnp.maximum(top_score, peak)
        merged_totals = None
        merged_output = None
        for peak, total, output in zip(peaks, totals, outputs):
            factor = jnp.exp(peak - top_score)
            t = total * factor
            o = output * widen(factor)
            merged_totals = t if merged_totals is None else merged_totals + t
            merged_output = o if merged_output is None else merged_output + o
        query_out = (merged_output / widen(merged_totals)).astype(jnp.bfloat16)
        return (block_out, query_out)

    return local


def solution(mesh):
    in_specs = (
        P(("groups", "ctx"), "head"),
        P(None, ("groups", "ctx"), "head"),
        P(None, ("groups", "ctx"), "head"),
        P(None, ("groups", "ctx"), "head"),
        P(("groups", "ctx")),
        P(("groups", "ctx"), "head"),
        P(None, ("groups", "ctx"), "head"),
        P("groups"),
    )
    out_specs = (P(("groups", "ctx"), "head"), P(("groups", "ctx"), "head"))
    return jax.shard_map(
        make_local(mesh.shape["ctx"]),
        mesh=mesh,
        in_specs=in_specs,
        out_specs=out_specs,
        check_vma=False,
    )
```

```python
import functools

import jax
import jax.numpy as jnp
from jax import lax
from jax.experimental import pallas as pl
from jax.experimental.pallas import tpu as pltpu
from jax.sharding import PartitionSpec as P

HD = 128


masked_score = -1e30


def widen(per_head):
    return jnp.repeat(per_head, HD, axis=-1)


def attention_kernel(masks, normalize, group_size, *refs):
    length_ref, q_ref = refs[0], refs[1]
    part_count = len(masks)
    kv_refs = refs[2 : 2 + 2 * part_count]
    rest = refs[2 + 2 * part_count :]
    if "pos" in masks:
        key_pos_ref, own_pos_ref = rest[0], rest[1]
        rest = rest[2:]
    out_refs = rest
    rows = q_ref.shape[0]
    scale = 1.0 / jnp.sqrt(jnp.float32(HD))
    visible = []
    for index, mask in enumerate(masks):
        key_count = kv_refs[2 * index].shape[0]
        if mask is None:
            visible.append(None)
        elif mask == "cache":
            cols = lax.broadcasted_iota(jnp.int32, (rows, key_count), 1)
            visible.append(cols < length_ref[0])
        elif mask == "causal":
            cols = lax.broadcasted_iota(jnp.int32, (rows, key_count), 1)
            row_ids = lax.broadcasted_iota(jnp.int32, (rows, key_count), 0)
            visible.append(cols <= row_ids)
        else:
            visible.append(key_pos_ref[...] <= own_pos_ref[...])
    for head in range(group_size):
        columns = slice(head * HD, (head + 1) * HD)
        q_head = q_ref[:, columns]
        all_scores = []
        for index in range(part_count):
            scores = lax.dot_general(
                q_head,
                kv_refs[2 * index][...],
                (((1,), (1,)), ((), ())),
                preferred_element_type=jnp.float32,
            ) * scale
            if visible[index] is not None:
                scores = jnp.where(visible[index], scores, masked_score)
            all_scores.append(scores)
        peak = jnp.max(all_scores[0], axis=1, keepdims=True)
        for scores in all_scores[1:]:
            peak = jnp.maximum(peak, jnp.max(scores, axis=1, keepdims=True))
        total = None
        output = None
        for index, scores in enumerate(all_scores):
            weights = jnp.exp(scores - peak)
            part_total = jnp.sum(weights, axis=1, keepdims=True)
            part_output = jnp.dot(
                weights.astype(jnp.bfloat16),
                kv_refs[2 * index + 1][...],
                preferred_element_type=jnp.float32,
            )
            total = part_total if total is None else total + part_total
            output = part_output if output is None else output + part_output
        if normalize:
            out_refs[0][:, columns] = (output / total).astype(out_refs[0].dtype)
        else:
            out_refs[0][:, columns] = output
            out_refs[1][:, columns] = jnp.broadcast_to(peak, (rows, HD))
            out_refs[2][:, columns] = jnp.broadcast_to(total, (rows, HD))


def attention(queries, parts, normalize, length=None, positions=None):
    rows, query_width = queries.shape
    kv_heads = parts[0][0].shape[2] // HD
    group_size = query_width // HD // kv_heads
    group_width = group_size * HD
    if length is None:
        length = jnp.zeros((1,), jnp.int32)
    masks = tuple(mask for _, mask in parts)
    in_specs = [pl.BlockSpec((rows, group_width), lambda g, n: (0, g))]
    operands = [queries]
    for pair, _ in parts:
        key_count = pair.shape[1]
        in_specs.append(pl.BlockSpec((pl.Squeezed(), key_count, HD), lambda g, n: (0, 0, g)))
        in_specs.append(pl.BlockSpec((pl.Squeezed(), key_count, HD), lambda g, n: (1, 0, g)))
        operands += [pair, pair]
    if positions is not None:
        key_pos = positions[0].reshape(1, -1)
        own_pos = positions[1].reshape(-1, 1)
        in_specs.append(pl.BlockSpec(key_pos.shape, lambda g, n: (0, 0)))
        in_specs.append(pl.BlockSpec(own_pos.shape, lambda g, n: (0, 0)))
        operands += [key_pos, own_pos]
    out_block = pl.BlockSpec((rows, group_width), lambda g, n: (0, g))
    if normalize:
        out_shape = [jax.ShapeDtypeStruct((rows, query_width), jnp.bfloat16)]
        out_specs = [out_block]
    else:
        out_shape = [jax.ShapeDtypeStruct((rows, query_width), jnp.float32)] * 3
        out_specs = [out_block] * 3
    return pl.pallas_call(
        functools.partial(attention_kernel, masks, normalize, group_size),
        grid_spec=pltpu.PrefetchScalarGridSpec(
            num_scalar_prefetch=1,
            grid=(kv_heads,),
            in_specs=in_specs,
            out_specs=out_specs,
        ),
        out_shape=out_shape,
    )(length, *operands)


def compact(wide):
    rows, width = wide.shape
    return wide.reshape(rows, width // HD, HD)[:, :, 0]


def shifted(value, shift, count):
    return lax.ppermute(value, "ctx", [(j, (j + shift) % count) for j in range(count)])


def make_local(ctx_count):
    def local(q_block, kv_block, anchor_kv, cache_kv, cache_len, query_q, query_kv, query_pos):
        me = lax.axis_index("ctx")
        own_count = query_q.shape[0]
        anchor_rows = anchor_kv.shape[1]
        width = kv_block.shape[2]
        pieces = (anchor_kv.reshape(-1), query_q.reshape(-1), query_kv.reshape(-1))
        sizes = [piece.shape[0] for piece in pieces]
        packed = jnp.concatenate(pieces)
        slots = [packed] + [shifted(packed, k, ctx_count) for k in range(1, ctx_count)]

        def unpack(slot):
            a = slot[: sizes[0]].reshape(2, anchor_rows, width)
            q = slot[sizes[0] : sizes[0] + sizes[1]].reshape(own_count, -1)
            kv = slot[sizes[0] + sizes[1] :].reshape(2, own_count, width)
            return a, q, kv

        unpacked = [unpack(slot) for slot in slots]
        anchor = jnp.concatenate([u[0] for u in unpacked], axis=1)
        all_queries = jnp.concatenate([u[1] for u in unpacked], axis=0)
        all_query_kv = jnp.concatenate([u[2] for u in unpacked], axis=1)
        slot_pos = jnp.concatenate(
            [
                lax.dynamic_slice_in_dim(query_pos, ((me - k) % ctx_count) * own_count, own_count)
                for k in range(ctx_count)
            ]
        )
        own_pos = slot_pos[:own_count]

        (block_out,) = attention(q_block, [(anchor, None), (kv_block, "causal")], True)

        context_output, context_peak, context_totals = attention(
            all_queries, [(cache_kv, "cache"), (kv_block, None)], False, length=cache_len
        )
        local_output, local_peak, local_totals = attention(
            query_q,
            [(anchor, None), (all_query_kv, "pos")],
            False,
            positions=(slot_pos, own_pos),
        )
        context_peak = compact(context_peak)
        context_totals = compact(context_totals)
        heads = context_peak.shape[1]
        context_packed = jnp.concatenate([context_output, context_peak, context_totals], axis=1)
        remote = [context_packed[:own_count]]
        for k in range(1, ctx_count):
            section = context_packed[k * own_count : (k + 1) * own_count]
            remote.append(shifted(section, -k, ctx_count))
        peaks = [compact(local_peak)] + [r[:, -2 * heads : -heads] for r in remote]
        totals = [compact(local_totals)] + [r[:, -heads:] for r in remote]
        outputs = [local_output] + [r[:, : -2 * heads] for r in remote]
        top_score = peaks[0]
        for peak in peaks[1:]:
            top_score = jnp.maximum(top_score, peak)
        merged_totals = None
        merged_output = None
        for peak, total, output in zip(peaks, totals, outputs):
            factor = jnp.exp(peak - top_score)
            t = total * factor
            o = output * widen(factor)
            merged_totals = t if merged_totals is None else merged_totals + t
            merged_output = o if merged_output is None else merged_output + o
        query_out = (merged_output / widen(merged_totals)).astype(jnp.bfloat16)
        return (block_out, query_out)

    return local


def solution(mesh):
    in_specs = (
        P(("groups", "ctx"), "head"),
        P(None, ("groups", "ctx"), "head"),
        P(None, ("groups", "ctx"), "head"),
        P(None, ("groups", "ctx"), "head"),
        P(("groups", "ctx")),
        P(("groups", "ctx"), "head"),
        P(None, ("groups", "ctx"), "head"),
        P("groups"),
    )
    out_specs = (P(("groups", "ctx"), "head"), P(("groups", "ctx"), "head"))
    return jax.shard_map(
        make_local(mesh.shape["ctx"]),
        mesh=mesh,
        in_specs=in_specs,
        out_specs=out_specs,
        check_vma=False,
    )
```

```python
import functools

import jax
import jax.numpy as jnp
from jax import lax
from jax.experimental import pallas as pl
from jax.experimental.pallas import tpu as pltpu
from jax.sharding import PartitionSpec as P

HD = 128


masked_score = -1e30


def widen(per_head):
    return jnp.repeat(per_head, HD, axis=-1)


def chunk_size(rows, key_count):
    size = min(key_count, max(128, 32768 // rows))
    while key_count % size:
        size //= 2
    return size


def attention_kernel(masks, normalize, rows, group_size, *refs):
    length_ref, q_ref = refs[0], refs[1]
    part_count = len(masks)
    kv_refs = refs[2 : 2 + 2 * part_count]
    rest = refs[2 + 2 * part_count :]
    if "pos" in masks:
        key_pos_ref, own_pos_ref = rest[0], rest[1]
        rest = rest[2:]
    out_ref = rest[0]
    side_ref = rest[1] if len(rest) > 1 else None
    scale = 1.0 / jnp.sqrt(jnp.float32(HD))
    stack = max(1, min(group_size, 512 // rows))
    for first in range(0, group_size, stack):
        heads = list(range(first, min(group_size, first + stack)))
        lhs = jnp.concatenate([q_ref[:, h * HD : (h + 1) * HD] for h in heads], axis=0)
        m_rows = lhs.shape[0]

        def chunk_visible(index, start, size):
            mask = masks[index]
            if mask is None:
                return None
            cols = start + lax.broadcasted_iota(jnp.int32, (m_rows, size), 1)
            if mask == "cache":
                return cols < length_ref[0]
            if mask == "causal":
                tokens = lax.broadcasted_iota(jnp.int32, (m_rows, size), 0)
                if m_rows > rows:
                    tokens = lax.rem(tokens, rows)
                return cols <= tokens
            own = own_pos_ref[...]
            if m_rows > rows:
                own = jnp.concatenate([own] * (m_rows // rows), axis=0)
            return key_pos_ref[:, pl.ds(start, size)] <= own

        def raw_scores(index, start, size):
            keys = kv_refs[2 * index][pl.ds(start, size), :]
            return lax.dot_general(
                lhs, keys, (((1,), (1,)), ((), ())), preferred_element_type=jnp.float32
            )

        def over_chunks(index, body, carry):
            key_count = kv_refs[2 * index].shape[0]
            size = chunk_size(m_rows, key_count)
            count = key_count // size

            def step(c, carry):
                start = pl.multiple_of(c * size, size)
                return body(index, start, size, carry)

            if count == 1:
                return step(0, carry)
            return lax.fori_loop(0, count, step, carry)

        def max_body(index, start, size, peak):
            raw = raw_scores(index, start, size)
            visible = chunk_visible(index, start, size)
            if visible is not None:
                raw = jnp.where(visible, raw, -jnp.inf)
            return jnp.maximum(peak, jnp.max(raw, axis=1, keepdims=True))

        peak = jnp.full((m_rows, 1), -jnp.inf, jnp.float32)
        for index in range(part_count):
            peak = over_chunks(index, max_body, peak)
        peak = peak * scale

        def sum_body(index, start, size, carry):
            total, output = carry
            scores = raw_scores(index, start, size) * scale
            visible = chunk_visible(index, start, size)
            if visible is not None:
                scores = jnp.where(visible, scores, masked_score)
            weights = jnp.exp(scores - peak)
            total = total + jnp.sum(weights, axis=1, keepdims=True)
            values = kv_refs[2 * index + 1][pl.ds(start, size), :]
            output = output + jnp.dot(
                weights.astype(jnp.bfloat16), values, preferred_element_type=jnp.float32
            )
            return total, output

        carry = (jnp.zeros((m_rows, 1), jnp.float32), jnp.zeros((m_rows, HD), jnp.float32))
        for index in range(part_count):
            carry = over_chunks(index, sum_body, carry)
        total, output = carry
        for slot, h in enumerate(heads):
            rows_of = slice(slot * rows, (slot + 1) * rows)
            if normalize:
                out_ref[:, h * HD : (h + 1) * HD] = (output[rows_of] / total[rows_of]).astype(
                    out_ref.dtype
                )
            else:
                out_ref[:, h * HD : (h + 1) * HD] = output[rows_of]
                side_ref[:, h : h + 1] = peak[rows_of]
                side_ref[:, HD // 2 + h : HD // 2 + h + 1] = total[rows_of]


def attention(queries, parts, normalize, length=None, positions=None):
    rows, query_width = queries.shape
    kv_heads = parts[0][0].shape[2] // HD
    group_size = query_width // HD // kv_heads
    group_width = group_size * HD
    if length is None:
        length = jnp.zeros((1,), jnp.int32)
    masks = tuple(mask for _, mask in parts)
    in_specs = [pl.BlockSpec((rows, group_width), lambda g, n: (0, g))]
    operands = [queries]
    for pair, _ in parts:
        key_count = pair.shape[1]
        in_specs.append(pl.BlockSpec((pl.Squeezed(), key_count, HD), lambda g, n: (0, 0, g)))
        in_specs.append(pl.BlockSpec((pl.Squeezed(), key_count, HD), lambda g, n: (1, 0, g)))
        operands += [pair, pair]
    if positions is not None:
        key_pos = positions[0].reshape(1, -1)
        own_pos = positions[1].reshape(-1, 1)
        in_specs.append(pl.BlockSpec(key_pos.shape, lambda g, n: (0, 0)))
        in_specs.append(pl.BlockSpec(own_pos.shape, lambda g, n: (0, 0)))
        operands += [key_pos, own_pos]
    out_shape = [
        jax.ShapeDtypeStruct((rows, query_width), jnp.bfloat16 if normalize else jnp.float32)
    ]
    out_specs = [pl.BlockSpec((rows, group_width), lambda g, n: (0, g))]
    if not normalize:
        out_shape.append(jax.ShapeDtypeStruct((kv_heads, rows, HD), jnp.float32))
        out_specs.append(pl.BlockSpec((pl.Squeezed(), rows, HD), lambda g, n: (g, 0, 0)))
    return pl.pallas_call(
        functools.partial(attention_kernel, masks, normalize, rows, group_size),
        grid_spec=pltpu.PrefetchScalarGridSpec(
            num_scalar_prefetch=1,
            grid=(kv_heads,),
            in_specs=in_specs,
            out_specs=out_specs,
        ),
        out_shape=out_shape,
    )(length, *operands)


def shifted(value, shift, count):
    return lax.ppermute(value, "ctx", [(j, (j + shift) % count) for j in range(count)])


def make_local(ctx_count):
    def local(q_block, kv_block, anchor_kv, cache_kv, cache_len, query_q, query_kv, query_pos):
        me = lax.axis_index("ctx")
        own_count = query_q.shape[0]
        width = kv_block.shape[2]
        query_width = query_q.shape[1]
        kv_heads = width // HD
        group_size = query_width // HD // kv_heads
        packed = jnp.concatenate([query_q.reshape(-1), query_kv.reshape(-1)])
        query_slots = [packed] + [shifted(packed, k, ctx_count) for k in range(1, ctx_count)]
        anchor_slots = [anchor_kv] + [shifted(anchor_kv, k, ctx_count) for k in range(1, ctx_count)]
        split = own_count * query_width
        all_queries = jnp.concatenate(
            [slot[:split].reshape(own_count, query_width) for slot in query_slots], axis=0
        )
        all_query_kv = jnp.concatenate(
            [slot[split:].reshape(2, own_count, width) for slot in query_slots], axis=1
        )
        anchor = jnp.concatenate(anchor_slots, axis=1)
        slot_pos = jnp.concatenate(
            [
                lax.dynamic_slice_in_dim(query_pos, ((me - k) % ctx_count) * own_count, own_count)
                for k in range(ctx_count)
            ]
        )
        own_pos = slot_pos[:own_count]

        context_output, context_side = attention(
            all_queries, [(cache_kv, "cache"), (kv_block, None)], False, length=cache_len
        )
        remote = [(context_output[:own_count], context_side[:, :own_count])]
        for k in range(1, ctx_count):
            rows = slice(k * own_count, (k + 1) * own_count)
            remote.append(shifted((context_output[rows], context_side[:, rows]), -k, ctx_count))

        (block_out,) = attention(q_block, [(anchor, None), (kv_block, "causal")], True)
        local_output, local_side = attention(
            query_q,
            [(anchor, None), (all_query_kv, "pos")],
            False,
            positions=(slot_pos, own_pos),
        )

        def per_head(side, first):
            picked = side[:, :, first : first + group_size]
            return jnp.transpose(picked, (1, 0, 2)).reshape(own_count, kv_heads * group_size)

        parts = [(local_output, local_side)] + remote
        peaks = [per_head(side, 0) for _, side in parts]
        totals = [per_head(side, HD // 2) for _, side in parts]
        outputs = [output for output, _ in parts]
        top_score = peaks[0]
        for peak in peaks[1:]:
            top_score = jnp.maximum(top_score, peak)
        merged_totals = None
        merged_output = None
        for peak, total, output in zip(peaks, totals, outputs):
            factor = jnp.exp(peak - top_score)
            t = total * factor
            o = output * widen(factor)
            merged_totals = t if merged_totals is None else merged_totals + t
            merged_output = o if merged_output is None else merged_output + o
        query_out = (merged_output / widen(merged_totals)).astype(jnp.bfloat16)
        return (block_out, query_out)

    return local


def solution(mesh):
    in_specs = (
        P(("groups", "ctx"), "head"),
        P(None, ("groups", "ctx"), "head"),
        P(None, ("groups", "ctx"), "head"),
        P(None, ("groups", "ctx"), "head"),
        P(("groups", "ctx")),
        P(("groups", "ctx"), "head"),
        P(None, ("groups", "ctx"), "head"),
        P("groups"),
    )
    out_specs = (P(("groups", "ctx"), "head"), P(("groups", "ctx"), "head"))
    return jax.shard_map(
        make_local(mesh.shape["ctx"]),
        mesh=mesh,
        in_specs=in_specs,
        out_specs=out_specs,
        check_vma=False,
    )
```

```python
import functools

import jax
import jax.numpy as jnp
from jax import lax
from jax.experimental import pallas as pl
from jax.experimental.pallas import tpu as pltpu
from jax.sharding import PartitionSpec as P

HD = 128


masked_score = -1e30


def widen(per_head):
    return jnp.repeat(per_head, HD, axis=-1)


STACK_ROWS = 512


def attention_kernel(masks, normalize, rows, group_size, *refs):
    length_ref, q_ref = refs[0], refs[1]
    part_count = len(masks)
    kv_refs = refs[2 : 2 + 2 * part_count]
    rest = refs[2 + 2 * part_count :]
    if "pos" in masks:
        key_pos_ref, own_pos_ref = rest[0], rest[1]
        rest = rest[2:]
    out_ref = rest[0]
    side_ref = None if normalize else rest[1]
    scale = 1.0 / jnp.sqrt(jnp.float32(HD))
    stack = max(1, min(group_size, STACK_ROWS // rows))
    visible = []
    for index, mask in enumerate(masks):
        key_count = kv_refs[2 * index].shape[0]
        shape = (rows * stack, key_count)
        if mask is None:
            visible.append(None)
        elif mask == "cache":
            cols = lax.broadcasted_iota(jnp.int32, shape, 1)
            visible.append(cols < length_ref[0])
        elif mask == "causal":
            cols = lax.broadcasted_iota(jnp.int32, shape, 1)
            tokens = lax.broadcasted_iota(jnp.int32, shape, 0)
            if stack > 1:
                tokens = lax.rem(tokens, rows)
            visible.append(cols <= tokens)
        else:
            own = own_pos_ref[...]
            if stack > 1:
                own = jnp.concatenate([own] * stack, axis=0)
            visible.append(key_pos_ref[...] <= own)
    for first in range(0, group_size, stack):
        heads = list(range(first, min(group_size, first + stack)))
        if len(heads) == 1:
            lhs = q_ref[:, first * HD : (first + 1) * HD]
        else:
            lhs = jnp.concatenate([q_ref[:, h * HD : (h + 1) * HD] for h in heads], axis=0)
        m_rows = lhs.shape[0]
        all_scores = []
        for index in range(part_count):
            scores = lax.dot_general(
                lhs,
                kv_refs[2 * index][...],
                (((1,), (1,)), ((), ())),
                preferred_element_type=jnp.float32,
            ) * scale
            if visible[index] is not None:
                scores = jnp.where(visible[index][:m_rows], scores, masked_score)
            all_scores.append(scores)
        peak = jnp.max(all_scores[0], axis=1, keepdims=True)
        for scores in all_scores[1:]:
            peak = jnp.maximum(peak, jnp.max(scores, axis=1, keepdims=True))
        total = None
        output = None
        for index, scores in enumerate(all_scores):
            weights = jnp.exp(scores - peak)
            part_total = jnp.sum(weights, axis=1, keepdims=True)
            part_output = jnp.dot(
                weights.astype(jnp.bfloat16),
                kv_refs[2 * index + 1][...],
                preferred_element_type=jnp.float32,
            )
            total = part_total if total is None else total + part_total
            output = part_output if output is None else output + part_output
        for slot, h in enumerate(heads):
            rows_of = slice(slot * rows, (slot + 1) * rows)
            if normalize:
                out_ref[:, h * HD : (h + 1) * HD] = (output[rows_of] / total[rows_of]).astype(
                    out_ref.dtype
                )
            else:
                out_ref[:, h * HD : (h + 1) * HD] = output[rows_of]
                side_ref[:, h : h + 1] = peak[rows_of]
                side_ref[:, HD // 2 + h : HD // 2 + h + 1] = total[rows_of]


def attention(queries, parts, normalize, length=None, positions=None):
    rows, query_width = queries.shape
    kv_heads = parts[0][0].shape[2] // HD
    group_size = query_width // HD // kv_heads
    group_width = group_size * HD
    if length is None:
        length = jnp.zeros((1,), jnp.int32)
    masks = tuple(mask for _, mask in parts)
    in_specs = [pl.BlockSpec((rows, group_width), lambda g, n: (0, g))]
    operands = [queries]
    for pair, _ in parts:
        key_count = pair.shape[1]
        in_specs.append(pl.BlockSpec((pl.Squeezed(), key_count, HD), lambda g, n: (0, 0, g)))
        in_specs.append(pl.BlockSpec((pl.Squeezed(), key_count, HD), lambda g, n: (1, 0, g)))
        operands += [pair, pair]
    if positions is not None:
        key_pos = positions[0].reshape(1, -1)
        own_pos = positions[1].reshape(-1, 1)
        in_specs.append(pl.BlockSpec(key_pos.shape, lambda g, n: (0, 0)))
        in_specs.append(pl.BlockSpec(own_pos.shape, lambda g, n: (0, 0)))
        operands += [key_pos, own_pos]
    out_shape = [
        jax.ShapeDtypeStruct((rows, query_width), jnp.bfloat16 if normalize else jnp.float32)
    ]
    out_specs = [pl.BlockSpec((rows, group_width), lambda g, n: (0, g))]
    if not normalize:
        out_shape.append(jax.ShapeDtypeStruct((kv_heads, rows, HD), jnp.float32))
        out_specs.append(pl.BlockSpec((pl.Squeezed(), rows, HD), lambda g, n: (g, 0, 0)))
    return pl.pallas_call(
        functools.partial(attention_kernel, masks, normalize, rows, group_size),
        grid_spec=pltpu.PrefetchScalarGridSpec(
            num_scalar_prefetch=1,
            grid=(kv_heads,),
            in_specs=in_specs,
            out_specs=out_specs,
        ),
        out_shape=out_shape,
    )(length, *operands)


def shifted(value, shift, count):
    return lax.ppermute(value, "ctx", [(j, (j + shift) % count) for j in range(count)])


def make_local(ctx_count):
    def local(q_block, kv_block, anchor_kv, cache_kv, cache_len, query_q, query_kv, query_pos):
        me = lax.axis_index("ctx")
        own_count = query_q.shape[0]
        width = kv_block.shape[2]
        query_width = query_q.shape[1]
        kv_heads = width // HD
        group_size = query_width // HD // kv_heads
        packed = jnp.concatenate([query_q.reshape(-1), query_kv.reshape(-1)])
        query_slots = [packed] + [shifted(packed, k, ctx_count) for k in range(1, ctx_count)]
        anchor_slots = [anchor_kv] + [shifted(anchor_kv, k, ctx_count) for k in range(1, ctx_count)]
        split = own_count * query_width
        all_queries = jnp.concatenate(
            [slot[:split].reshape(own_count, query_width) for slot in query_slots], axis=0
        )
        all_query_kv = jnp.concatenate(
            [slot[split:].reshape(2, own_count, width) for slot in query_slots], axis=1
        )
        anchor = jnp.concatenate(anchor_slots, axis=1)
        slot_pos = jnp.concatenate(
            [
                lax.dynamic_slice_in_dim(query_pos, ((me - k) % ctx_count) * own_count, own_count)
                for k in range(ctx_count)
            ]
        )
        own_pos = slot_pos[:own_count]

        context_output, context_side = attention(
            all_queries, [(cache_kv, "cache"), (kv_block, None)], False, length=cache_len
        )
        remote = [(context_output[:own_count], context_side[:, :own_count])]
        for k in range(1, ctx_count):
            rows = slice(k * own_count, (k + 1) * own_count)
            remote.append(shifted((context_output[rows], context_side[:, rows]), -k, ctx_count))

        (block_out,) = attention(q_block, [(anchor, None), (kv_block, "causal")], True)
        local_output, local_side = attention(
            query_q,
            [(anchor, None), (all_query_kv, "pos")],
            False,
            positions=(slot_pos, own_pos),
        )

        def per_head(side, first):
            picked = side[:, :, first : first + group_size]
            return jnp.transpose(picked, (1, 0, 2)).reshape(own_count, kv_heads * group_size)

        parts = [(local_output, local_side)] + remote
        peaks = [per_head(side, 0) for _, side in parts]
        totals = [per_head(side, HD // 2) for _, side in parts]
        outputs = [output for output, _ in parts]
        top_score = peaks[0]
        for peak in peaks[1:]:
            top_score = jnp.maximum(top_score, peak)
        merged_totals = None
        merged_output = None
        for peak, total, output in zip(peaks, totals, outputs):
            factor = jnp.exp(peak - top_score)
            t = total * factor
            o = output * widen(factor)
            merged_totals = t if merged_totals is None else merged_totals + t
            merged_output = o if merged_output is None else merged_output + o
        query_out = (merged_output / widen(merged_totals)).astype(jnp.bfloat16)
        return (block_out, query_out)

    return local


def solution(mesh):
    in_specs = (
        P(("groups", "ctx"), "head"),
        P(None, ("groups", "ctx"), "head"),
        P(None, ("groups", "ctx"), "head"),
        P(None, ("groups", "ctx"), "head"),
        P(("groups", "ctx")),
        P(("groups", "ctx"), "head"),
        P(None, ("groups", "ctx"), "head"),
        P("groups"),
    )
    out_specs = (P(("groups", "ctx"), "head"), P(("groups", "ctx"), "head"))
    return jax.shard_map(
        make_local(mesh.shape["ctx"]),
        mesh=mesh,
        in_specs=in_specs,
        out_specs=out_specs,
        check_vma=False,
    )
```

```python
import functools

import jax
import jax.numpy as jnp
from jax import lax
from jax.experimental import pallas as pl
from jax.experimental.pallas import tpu as pltpu
from jax.sharding import PartitionSpec as P

HD = 128


masked_score = -1e30


def widen(per_head):
    return jnp.repeat(per_head, HD, axis=-1)


STACK_ROWS = 512


def attention_kernel(masks, normalize, rows, group_size, *refs):
    length_ref, q_ref = refs[0], refs[1]
    part_count = len(masks)
    kv_refs = refs[2 : 2 + 2 * part_count]
    rest = refs[2 + 2 * part_count :]
    if "pos" in masks:
        key_pos_ref, own_pos_ref = rest[0], rest[1]
        rest = rest[2:]
    out_ref = rest[0]
    side_ref = None if normalize else rest[1]
    scale = 1.0 / jnp.sqrt(jnp.float32(HD))
    stack = max(1, min(group_size, STACK_ROWS // rows))
    visible = []
    for index, mask in enumerate(masks):
        key_count = kv_refs[2 * index].shape[0]
        shape = (rows * stack, key_count)
        if mask is None:
            visible.append(None)
        elif mask == "cache":
            cols = lax.broadcasted_iota(jnp.int32, shape, 1)
            visible.append(cols < length_ref[0])
        elif mask == "causal":
            cols = lax.broadcasted_iota(jnp.int32, shape, 1)
            tokens = lax.broadcasted_iota(jnp.int32, shape, 0)
            if stack > 1:
                tokens = lax.rem(tokens, rows)
            visible.append(cols <= tokens)
        else:
            own = own_pos_ref[...]
            if stack > 1:
                own = jnp.concatenate([own] * stack, axis=0)
            visible.append(key_pos_ref[...] <= own)
    for first in range(0, group_size, stack):
        heads = list(range(first, min(group_size, first + stack)))
        if len(heads) == 1:
            lhs = q_ref[:, first * HD : (first + 1) * HD]
        else:
            lhs = jnp.concatenate([q_ref[:, h * HD : (h + 1) * HD] for h in heads], axis=0)
        m_rows = lhs.shape[0]
        all_scores = []
        for index in range(part_count):
            scores = lax.dot_general(
                lhs,
                kv_refs[2 * index][...],
                (((1,), (1,)), ((), ())),
                preferred_element_type=jnp.float32,
            ) * scale
            if visible[index] is not None:
                scores = jnp.where(visible[index][:m_rows], scores, masked_score)
            all_scores.append(scores)
        peak = jnp.max(all_scores[0], axis=1, keepdims=True)
        for scores in all_scores[1:]:
            peak = jnp.maximum(peak, jnp.max(scores, axis=1, keepdims=True))
        total = None
        output = None
        for index, scores in enumerate(all_scores):
            weights = jnp.exp(scores - peak)
            part_total = jnp.sum(weights, axis=1, keepdims=True)
            part_output = jnp.dot(
                weights.astype(jnp.bfloat16),
                kv_refs[2 * index + 1][...],
                preferred_element_type=jnp.float32,
            )
            total = part_total if total is None else total + part_total
            output = part_output if output is None else output + part_output
        for slot, h in enumerate(heads):
            rows_of = slice(slot * rows, (slot + 1) * rows)
            if normalize:
                out_ref[:, h * HD : (h + 1) * HD] = (output[rows_of] / total[rows_of]).astype(
                    out_ref.dtype
                )
            else:
                out_ref[:, h * HD : (h + 1) * HD] = output[rows_of]
                side_ref[:, h : h + 1] = peak[rows_of]
                side_ref[:, HD // 2 + h : HD // 2 + h + 1] = total[rows_of]


def attention(queries, parts, normalize, length=None, positions=None):
    rows, query_width = queries.shape
    kv_heads = parts[0][0].shape[2] // HD
    group_size = query_width // HD // kv_heads
    group_width = group_size * HD
    if length is None:
        length = jnp.zeros((1,), jnp.int32)
    masks = tuple(mask for _, mask in parts)
    in_specs = [pl.BlockSpec((rows, group_width), lambda g, n: (0, g))]
    operands = [queries]
    for pair, _ in parts:
        key_count = pair.shape[1]
        in_specs.append(pl.BlockSpec((pl.Squeezed(), key_count, HD), lambda g, n: (0, 0, g)))
        in_specs.append(pl.BlockSpec((pl.Squeezed(), key_count, HD), lambda g, n: (1, 0, g)))
        operands += [pair, pair]
    if positions is not None:
        key_pos = positions[0].reshape(1, -1)
        own_pos = positions[1].reshape(-1, 1)
        in_specs.append(pl.BlockSpec(key_pos.shape, lambda g, n: (0, 0)))
        in_specs.append(pl.BlockSpec(own_pos.shape, lambda g, n: (0, 0)))
        operands += [key_pos, own_pos]
    out_shape = [
        jax.ShapeDtypeStruct((rows, query_width), jnp.bfloat16 if normalize else jnp.float32)
    ]
    out_specs = [pl.BlockSpec((rows, group_width), lambda g, n: (0, g))]
    if not normalize:
        out_shape.append(jax.ShapeDtypeStruct((kv_heads, rows, HD), jnp.float32))
        out_specs.append(pl.BlockSpec((pl.Squeezed(), rows, HD), lambda g, n: (g, 0, 0)))
    return pl.pallas_call(
        functools.partial(attention_kernel, masks, normalize, rows, group_size),
        grid_spec=pltpu.PrefetchScalarGridSpec(
            num_scalar_prefetch=1,
            grid=(kv_heads,),
            in_specs=in_specs,
            out_specs=out_specs,
        ),
        out_shape=out_shape,
    )(length, *operands)


def shifted(value, shift, count):
    return lax.ppermute(value, "ctx", [(j, (j + shift) % count) for j in range(count)])


def make_local(ctx_count):
    def local(q_block, kv_block, anchor_kv, cache_kv, cache_len, query_q, query_kv, query_pos):
        me = lax.axis_index("ctx")
        own_count = query_q.shape[0]
        width = kv_block.shape[2]
        query_width = query_q.shape[1]
        kv_heads = width // HD
        group_size = query_width // HD // kv_heads
        packed = jnp.concatenate([query_q.reshape(-1), query_kv.reshape(-1)])
        query_slots = [packed] + [shifted(packed, k, ctx_count) for k in range(1, ctx_count)]
        anchor_slots = [anchor_kv] + [shifted(anchor_kv, k, ctx_count) for k in range(1, ctx_count)]
        split = own_count * query_width
        all_queries = jnp.concatenate(
            [slot[:split].reshape(own_count, query_width) for slot in query_slots], axis=0
        )
        all_query_kv = jnp.concatenate(
            [slot[split:].reshape(2, own_count, width) for slot in query_slots], axis=1
        )
        anchor = jnp.concatenate(anchor_slots, axis=1)
        slot_pos = jnp.concatenate(
            [
                lax.dynamic_slice_in_dim(query_pos, ((me - k) % ctx_count) * own_count, own_count)
                for k in range(ctx_count)
            ]
        )
        own_pos = slot_pos[:own_count]

        context_output, context_side = attention(
            all_queries, [(cache_kv, "cache"), (kv_block, None)], False, length=cache_len
        )
        side_width = kv_heads * HD
        context_side = jnp.transpose(context_side, (1, 0, 2)).reshape(-1, side_width)
        context_packed = jnp.concatenate([context_output, context_side], axis=1)
        sections = [context_packed[:own_count]]
        for k in range(1, ctx_count):
            rows = slice(k * own_count, (k + 1) * own_count)
            sections.append(shifted(context_packed[rows], -k, ctx_count))
        remote = [
            (
                section[:, :query_width],
                jnp.transpose(section[:, query_width:].reshape(own_count, kv_heads, HD), (1, 0, 2)),
            )
            for section in sections
        ]

        (block_out,) = attention(q_block, [(anchor, None), (kv_block, "causal")], True)
        local_output, local_side = attention(
            query_q,
            [(anchor, None), (all_query_kv, "pos")],
            False,
            positions=(slot_pos, own_pos),
        )

        def per_head(side, first):
            picked = side[:, :, first : first + group_size]
            return jnp.transpose(picked, (1, 0, 2)).reshape(own_count, kv_heads * group_size)

        parts = [(local_output, local_side)] + remote
        peaks = [per_head(side, 0) for _, side in parts]
        totals = [per_head(side, HD // 2) for _, side in parts]
        outputs = [output for output, _ in parts]
        top_score = peaks[0]
        for peak in peaks[1:]:
            top_score = jnp.maximum(top_score, peak)
        merged_totals = None
        merged_output = None
        for peak, total, output in zip(peaks, totals, outputs):
            factor = jnp.exp(peak - top_score)
            t = total * factor
            o = output * widen(factor)
            merged_totals = t if merged_totals is None else merged_totals + t
            merged_output = o if merged_output is None else merged_output + o
        query_out = (merged_output / widen(merged_totals)).astype(jnp.bfloat16)
        return (block_out, query_out)

    return local


def solution(mesh):
    in_specs = (
        P(("groups", "ctx"), "head"),
        P(None, ("groups", "ctx"), "head"),
        P(None, ("groups", "ctx"), "head"),
        P(None, ("groups", "ctx"), "head"),
        P(("groups", "ctx")),
        P(("groups", "ctx"), "head"),
        P(None, ("groups", "ctx"), "head"),
        P("groups"),
    )
    out_specs = (P(("groups", "ctx"), "head"), P(("groups", "ctx"), "head"))
    return jax.shard_map(
        make_local(mesh.shape["ctx"]),
        mesh=mesh,
        in_specs=in_specs,
        out_specs=out_specs,
        check_vma=False,
    )
```

```python
import functools

import jax
import jax.numpy as jnp
from jax import lax
from jax.experimental import pallas as pl
from jax.experimental.pallas import tpu as pltpu
from jax.sharding import PartitionSpec as P

HD = 128


masked_score = -1e30


def widen(per_head):
    return jnp.repeat(per_head, HD, axis=-1)


STACK_ROWS = 512


def attention_kernel(masks, normalize, packed, rows, group_size, kv_heads, *refs):
    length_ref, q_ref = refs[0], refs[1]
    part_count = len(masks)
    kv_refs = refs[2 : 2 + 2 * part_count]
    rest = refs[2 + 2 * part_count :]
    if "pos" in masks:
        key_pos_ref, own_pos_ref = rest[0], rest[1]
        rest = rest[2:]
    out_ref = rest[0]
    side_ref = None if normalize or packed else rest[1]
    query_width = kv_heads * group_size * HD
    scale = 1.0 / jnp.sqrt(jnp.float32(HD))
    stack = max(1, min(group_size, STACK_ROWS // rows))
    visible = []
    for index, mask in enumerate(masks):
        key_count = kv_refs[2 * index].shape[0]
        shape = (rows * stack, key_count)
        if mask is None:
            visible.append(None)
        elif mask == "cache":
            cols = lax.broadcasted_iota(jnp.int32, shape, 1)
            visible.append(cols < length_ref[0])
        elif mask == "causal":
            cols = lax.broadcasted_iota(jnp.int32, shape, 1)
            tokens = lax.broadcasted_iota(jnp.int32, shape, 0)
            if stack > 1:
                tokens = lax.rem(tokens, rows)
            visible.append(cols <= tokens)
        else:
            own = own_pos_ref[...]
            if stack > 1:
                own = jnp.concatenate([own] * stack, axis=0)
            visible.append(key_pos_ref[...] <= own)
    for first in range(0, group_size, stack):
        heads = list(range(first, min(group_size, first + stack)))
        if len(heads) == 1:
            lhs = q_ref[:, first * HD : (first + 1) * HD]
        else:
            lhs = jnp.concatenate([q_ref[:, h * HD : (h + 1) * HD] for h in heads], axis=0)
        m_rows = lhs.shape[0]
        all_scores = []
        for index in range(part_count):
            raw = lax.dot_general(
                lhs,
                kv_refs[2 * index][...],
                (((1,), (1,)), ((), ())),
                preferred_element_type=jnp.float32,
            )
            if visible[index] is not None:
                raw = jnp.where(visible[index][:m_rows], raw, -jnp.inf)
            all_scores.append(raw)
        peak = jnp.max(all_scores[0], axis=1, keepdims=True)
        for raw in all_scores[1:]:
            peak = jnp.maximum(peak, jnp.max(raw, axis=1, keepdims=True))
        peak = peak * scale
        total = None
        output = None
        for index, raw in enumerate(all_scores):
            weights = jnp.exp(raw * scale - peak)
            part_total = jnp.sum(weights, axis=1, keepdims=True)
            part_output = jnp.dot(
                weights.astype(jnp.bfloat16),
                kv_refs[2 * index + 1][...],
                preferred_element_type=jnp.float32,
            )
            total = part_total if total is None else total + part_total
            output = part_output if output is None else output + part_output
        for slot, h in enumerate(heads):
            rows_of = slice(slot * rows, (slot + 1) * rows)
            if normalize:
                out_ref[:, h * HD : (h + 1) * HD] = (output[rows_of] / total[rows_of]).astype(
                    out_ref.dtype
                )
            elif packed:

                def store(gi, h=h, rows_of=rows_of):
                    head = gi * group_size + h
                    out_ref[:, head * HD : (head + 1) * HD] = output[rows_of]
                    side = query_width + gi * HD
                    out_ref[:, side + h : side + h + 1] = peak[rows_of]
                    side += HD // 2
                    out_ref[:, side + h : side + h + 1] = total[rows_of]

                for gi in range(kv_heads):
                    pl.when(pl.program_id(0) == gi)(functools.partial(store, gi))
            else:
                out_ref[:, h * HD : (h + 1) * HD] = output[rows_of]
                side_ref[:, h : h + 1] = peak[rows_of]
                side_ref[:, HD // 2 + h : HD // 2 + h + 1] = total[rows_of]


def attention(queries, parts, normalize, length=None, positions=None, packed=False):
    rows, query_width = queries.shape
    kv_heads = parts[0][0].shape[2] // HD
    group_size = query_width // HD // kv_heads
    group_width = group_size * HD
    if length is None:
        length = jnp.zeros((1,), jnp.int32)
    masks = tuple(mask for _, mask in parts)
    in_specs = [pl.BlockSpec((rows, group_width), lambda g, n: (0, g))]
    operands = [queries]
    for pair, _ in parts:
        key_count = pair.shape[1]
        in_specs.append(pl.BlockSpec((pl.Squeezed(), key_count, HD), lambda g, n: (0, 0, g)))
        in_specs.append(pl.BlockSpec((pl.Squeezed(), key_count, HD), lambda g, n: (1, 0, g)))
        operands += [pair, pair]
    if positions is not None:
        key_pos = positions[0].reshape(1, -1)
        own_pos = positions[1].reshape(-1, 1)
        in_specs.append(pl.BlockSpec(key_pos.shape, lambda g, n: (0, 0)))
        in_specs.append(pl.BlockSpec(own_pos.shape, lambda g, n: (0, 0)))
        operands += [key_pos, own_pos]
    out_shape = [
        jax.ShapeDtypeStruct((rows, query_width), jnp.bfloat16 if normalize else jnp.float32)
    ]
    out_specs = [pl.BlockSpec((rows, group_width), lambda g, n: (0, g))]
    if packed:
        full = (rows, query_width + kv_heads * HD)
        out_shape = [jax.ShapeDtypeStruct(full, jnp.float32)]
        out_specs = [pl.BlockSpec(full, lambda g, n: (0, 0))]
    elif not normalize:
        out_shape.append(jax.ShapeDtypeStruct((kv_heads, rows, HD), jnp.float32))
        out_specs.append(pl.BlockSpec((pl.Squeezed(), rows, HD), lambda g, n: (g, 0, 0)))
    return pl.pallas_call(
        functools.partial(attention_kernel, masks, normalize, packed, rows, group_size, kv_heads),
        grid_spec=pltpu.PrefetchScalarGridSpec(
            num_scalar_prefetch=1,
            grid=(kv_heads,),
            in_specs=in_specs,
            out_specs=out_specs,
        ),
        out_shape=out_shape,
    )(length, *operands)


def shifted(value, shift, count):
    return lax.ppermute(value, "ctx", [(j, (j + shift) % count) for j in range(count)])


def make_local(ctx_count):
    def local(q_block, kv_block, anchor_kv, cache_kv, cache_len, query_q, query_kv, query_pos):
        me = lax.axis_index("ctx")
        own_count = query_q.shape[0]
        width = kv_block.shape[2]
        query_width = query_q.shape[1]
        kv_heads = width // HD
        group_size = query_width // HD // kv_heads
        packed = jnp.concatenate([query_q.reshape(-1), query_kv.reshape(-1)])
        query_slots = [packed] + [shifted(packed, k, ctx_count) for k in range(1, ctx_count)]
        anchor_slots = [anchor_kv] + [shifted(anchor_kv, k, ctx_count) for k in range(1, ctx_count)]
        split = own_count * query_width
        all_queries = jnp.concatenate(
            [slot[:split].reshape(own_count, query_width) for slot in query_slots], axis=0
        )
        all_query_kv = jnp.concatenate(
            [slot[split:].reshape(2, own_count, width) for slot in query_slots], axis=1
        )
        anchor = jnp.concatenate(anchor_slots, axis=1)
        slot_pos = jnp.concatenate(
            [
                lax.dynamic_slice_in_dim(query_pos, ((me - k) % ctx_count) * own_count, own_count)
                for k in range(ctx_count)
            ]
        )
        own_pos = slot_pos[:own_count]

        (context_packed,) = attention(
            all_queries,
            [(cache_kv, "cache"), (kv_block, None)],
            False,
            length=cache_len,
            packed=True,
        )
        sections = [context_packed[:own_count]]
        for k in range(1, ctx_count):
            rows = slice(k * own_count, (k + 1) * own_count)
            sections.append(shifted(context_packed[rows], -k, ctx_count))
        remote = [
            (
                section[:, :query_width],
                jnp.transpose(section[:, query_width:].reshape(own_count, kv_heads, HD), (1, 0, 2)),
            )
            for section in sections
        ]

        (block_out,) = attention(q_block, [(anchor, None), (kv_block, "causal")], True)
        local_output, local_side = attention(
            query_q,
            [(anchor, None), (all_query_kv, "pos")],
            False,
            positions=(slot_pos, own_pos),
        )

        def per_head(side, first):
            picked = side[:, :, first : first + group_size]
            return jnp.transpose(picked, (1, 0, 2)).reshape(own_count, kv_heads * group_size)

        parts = [(local_output, local_side)] + remote
        peaks = [per_head(side, 0) for _, side in parts]
        totals = [per_head(side, HD // 2) for _, side in parts]
        outputs = [output for output, _ in parts]
        top_score = peaks[0]
        for peak in peaks[1:]:
            top_score = jnp.maximum(top_score, peak)
        merged_totals = None
        merged_output = None
        for peak, total, output in zip(peaks, totals, outputs):
            factor = jnp.exp(peak - top_score)
            t = total * factor
            o = output * widen(factor)
            merged_totals = t if merged_totals is None else merged_totals + t
            merged_output = o if merged_output is None else merged_output + o
        query_out = (merged_output / widen(merged_totals)).astype(jnp.bfloat16)
        return (block_out, query_out)

    return local


def solution(mesh):
    in_specs = (
        P(("groups", "ctx"), "head"),
        P(None, ("groups", "ctx"), "head"),
        P(None, ("groups", "ctx"), "head"),
        P(None, ("groups", "ctx"), "head"),
        P(("groups", "ctx")),
        P(("groups", "ctx"), "head"),
        P(None, ("groups", "ctx"), "head"),
        P("groups"),
    )
    out_specs = (P(("groups", "ctx"), "head"), P(("groups", "ctx"), "head"))
    return jax.shard_map(
        make_local(mesh.shape["ctx"]),
        mesh=mesh,
        in_specs=in_specs,
        out_specs=out_specs,
        check_vma=False,
    )
```

```python
import functools

import jax
import jax.numpy as jnp
from jax import lax
from jax.experimental import pallas as pl
from jax.experimental.pallas import tpu as pltpu
from jax.sharding import PartitionSpec as P

HD = 128
STACK_ROWS = 512


masked_score = -1e30


def widen(per_head):
    return jnp.repeat(per_head, HD, axis=-1)


def attention_kernel(masks, slots, normalize, packed, group_size, kv_heads, ctx_count, query_count, *refs):
    scalar_ref = refs[0]
    q_refs = refs[1 : 1 + query_count]
    part_count = len(masks)
    kv_refs = refs[1 + query_count : 1 + query_count + 2 * part_count]
    rest = refs[1 + query_count + 2 * part_count :]
    if "pos" in masks:
        pos_ref = rest[0]
        rest = rest[1:]
    out_ref = rest[0]
    side_ref = None if normalize or packed else rest[1]
    query_width = kv_heads * group_size * HD
    slot_rows = q_refs[0].shape[0]
    rows = slot_rows * query_count
    scale = 1.0 / jnp.sqrt(jnp.float32(HD))
    stack = max(1, min(group_size, STACK_ROWS // rows))
    visible = []
    if "pos" in masks:
        own_row = pos_ref[pl.ds(scalar_ref[1], 1), :]
        eye = lax.broadcasted_iota(jnp.int32, (rows, rows), 0) == lax.broadcasted_iota(
            jnp.int32, (rows, rows), 1
        )
        own_col = jnp.sum(
            jnp.where(eye, jnp.broadcast_to(own_row, (rows, rows)), 0), axis=1, keepdims=True
        )
        if stack > 1:
            own_col = jnp.concatenate([own_col] * stack, axis=0)
    for index, mask in enumerate(masks):
        key_count = kv_refs[2 * index].shape[0]
        shape = (rows * stack, key_count)
        if mask is None:
            visible.append(None)
        elif mask == "cache":
            cols = lax.broadcasted_iota(jnp.int32, shape, 1)
            visible.append(cols < scalar_ref[0])
        elif mask == "causal":
            cols = lax.broadcasted_iota(jnp.int32, shape, 1)
            tokens = lax.broadcasted_iota(jnp.int32, shape, 0)
            if stack > 1:
                tokens = lax.rem(tokens, rows)
            visible.append(cols <= tokens)
        else:
            source = lax.rem(scalar_ref[1] + (ctx_count - slots[index]), ctx_count)
            key_row = pos_ref[pl.ds(source, 1), :]
            visible.append(key_row <= own_col)
    for first in range(0, group_size, stack):
        heads = list(range(first, min(group_size, first + stack)))
        pieces = [q_ref[:, h * HD : (h + 1) * HD] for h in heads for q_ref in q_refs]
        lhs = pieces[0] if len(pieces) == 1 else jnp.concatenate(pieces, axis=0)
        m_rows = lhs.shape[0]
        all_scores = []
        for index in range(part_count):
            raw = lax.dot_general(
                lhs,
                kv_refs[2 * index][...],
                (((1,), (1,)), ((), ())),
                preferred_element_type=jnp.float32,
            )
            if visible[index] is not None:
                raw = jnp.where(visible[index][:m_rows], raw, -jnp.inf)
            all_scores.append(raw)
        peak = jnp.max(all_scores[0], axis=1, keepdims=True)
        for raw in all_scores[1:]:
            peak = jnp.maximum(peak, jnp.max(raw, axis=1, keepdims=True))
        peak = peak * scale
        total = None
        output = None
        for index, raw in enumerate(all_scores):
            weights = jnp.exp(raw * scale - peak)
            part_total = jnp.sum(weights, axis=1, keepdims=True)
            part_output = jnp.dot(
                weights.astype(jnp.bfloat16),
                kv_refs[2 * index + 1][...],
                preferred_element_type=jnp.float32,
            )
            total = part_total if total is None else total + part_total
            output = part_output if output is None else output + part_output
        for slot, h in enumerate(heads):
            rows_of = slice(slot * rows, (slot + 1) * rows)
            if normalize:
                out_ref[:, h * HD : (h + 1) * HD] = (output[rows_of] / total[rows_of]).astype(
                    out_ref.dtype
                )
            elif packed:

                def store(gi, h=h, rows_of=rows_of):
                    head = gi * group_size + h
                    out_ref[:, head * HD : (head + 1) * HD] = output[rows_of]
                    side = query_width + gi * HD
                    out_ref[:, side + h : side + h + 1] = peak[rows_of]
                    side += HD // 2
                    out_ref[:, side + h : side + h + 1] = total[rows_of]

                for gi in range(kv_heads):
                    pl.when(pl.program_id(0) == gi)(functools.partial(store, gi))
            else:
                out_ref[:, h * HD : (h + 1) * HD] = output[rows_of]
                side_ref[:, h : h + 1] = peak[rows_of]
                side_ref[:, HD // 2 + h : HD // 2 + h + 1] = total[rows_of]


def attention(query_slots, parts, normalize, scalars, query_width, pos=None, packed=False):
    slot_rows = query_slots[0].shape[0]
    rows = slot_rows * len(query_slots)
    if parts[0][1] == "pos":
        kv_width = (parts[0][0].shape[1] - query_width) // 2
    else:
        kv_width = parts[0][0].shape[-1]
    kv_heads = kv_width // HD
    group_size = query_width // HD // kv_heads
    group_width = group_size * HD
    masks = tuple(part[1] for part in parts)
    slots = tuple(part[2] if len(part) > 2 else None for part in parts)
    in_specs = [pl.BlockSpec((slot_rows, group_width), lambda g, s: (0, g)) for _ in query_slots]
    operands = list(query_slots)
    for part in parts:
        array = part[0]
        if part[1] == "pos":
            first = query_width // HD
            in_specs.append(pl.BlockSpec((array.shape[0], HD), lambda g, s, c=first: (0, c + g)))
            in_specs.append(
                pl.BlockSpec((array.shape[0], HD), lambda g, s, c=first + kv_heads: (0, c + g))
            )
        else:
            key_count = array.shape[1]
            in_specs.append(pl.BlockSpec((pl.Squeezed(), key_count, HD), lambda g, s: (0, 0, g)))
            in_specs.append(pl.BlockSpec((pl.Squeezed(), key_count, HD), lambda g, s: (1, 0, g)))
        operands += [array, array]
    ctx_count = 1
    if pos is not None:
        ctx_count = pos.shape[0]
        in_specs.append(pl.BlockSpec(pos.shape, lambda g, s: (0, 0)))
        operands.append(pos)
    out_shape = [
        jax.ShapeDtypeStruct((rows, query_width), jnp.bfloat16 if normalize else jnp.float32)
    ]
    out_specs = [pl.BlockSpec((rows, group_width), lambda g, s: (0, g))]
    if packed:
        full = (rows, query_width + kv_heads * HD)
        out_shape = [jax.ShapeDtypeStruct(full, jnp.float32)]
        out_specs = [pl.BlockSpec(full, lambda g, s: (0, 0))]
    elif not normalize:
        out_shape.append(jax.ShapeDtypeStruct((kv_heads, rows, HD), jnp.float32))
        out_specs.append(pl.BlockSpec((pl.Squeezed(), rows, HD), lambda g, s: (g, 0, 0)))
    kernel = functools.partial(
        attention_kernel,
        masks,
        slots,
        normalize,
        packed,
        group_size,
        kv_heads,
        ctx_count,
        len(query_slots),
    )
    return pl.pallas_call(
        kernel,
        grid_spec=pltpu.PrefetchScalarGridSpec(
            num_scalar_prefetch=1,
            grid=(kv_heads,),
            in_specs=in_specs,
            out_specs=out_specs,
        ),
        out_shape=out_shape,
    )(scalars, *operands)


def shifted(value, shift, count):
    return lax.ppermute(value, "ctx", [(j, (j + shift) % count) for j in range(count)])


def make_local(ctx_count):
    def local(q_block, kv_block, anchor_kv, cache_kv, cache_len, query_q, query_kv, query_pos):
        me = lax.axis_index("ctx")
        own_count = query_q.shape[0]
        width = kv_block.shape[2]
        query_width = query_q.shape[1]
        kv_heads = width // HD
        group_size = query_width // HD // kv_heads
        packed = jnp.concatenate([query_q, query_kv[0], query_kv[1]], axis=1)
        query_slots = [packed] + [shifted(packed, k, ctx_count) for k in range(1, ctx_count)]
        anchor_slots = [anchor_kv] + [shifted(anchor_kv, k, ctx_count) for k in range(1, ctx_count)]
        scalars = jnp.stack([cache_len[0], me.astype(jnp.int32)])
        positions = query_pos.reshape(ctx_count, own_count)

        (context_packed,) = attention(
            query_slots,
            [(cache_kv, "cache"), (kv_block, None)],
            False,
            scalars,
            query_width,
            packed=True,
        )
        sections = [context_packed[:own_count]]
        for k in range(1, ctx_count):
            rows = slice(k * own_count, (k + 1) * own_count)
            sections.append(shifted(context_packed[rows], -k, ctx_count))
        remote = [
            (
                section[:, :query_width],
                jnp.transpose(section[:, query_width:].reshape(own_count, kv_heads, HD), (1, 0, 2)),
            )
            for section in sections
        ]

        anchor_parts = [(slot, None) for slot in anchor_slots]
        (block_out,) = attention(
            [q_block], anchor_parts + [(kv_block, "causal")], True, scalars, query_width
        )
        local_output, local_side = attention(
            [query_q],
            anchor_parts + [(slot, "pos", k) for k, slot in enumerate(query_slots)],
            False,
            scalars,
            query_width,
            pos=positions,
        )

        def per_head(side, first):
            picked = side[:, :, first : first + group_size]
            return jnp.transpose(picked, (1, 0, 2)).reshape(own_count, kv_heads * group_size)

        parts = [(local_output, local_side)] + remote
        peaks = [per_head(side, 0) for _, side in parts]
        totals = [per_head(side, HD // 2) for _, side in parts]
        outputs = [output for output, _ in parts]
        top_score = peaks[0]
        for peak in peaks[1:]:
            top_score = jnp.maximum(top_score, peak)
        merged_totals = None
        merged_output = None
        for peak, total, output in zip(peaks, totals, outputs):
            factor = jnp.exp(peak - top_score)
            t = total * factor
            o = output * widen(factor)
            merged_totals = t if merged_totals is None else merged_totals + t
            merged_output = o if merged_output is None else merged_output + o
        query_out = (merged_output / widen(merged_totals)).astype(jnp.bfloat16)
        return (block_out, query_out)

    return local


def solution(mesh):
    in_specs = (
        P(("groups", "ctx"), "head"),
        P(None, ("groups", "ctx"), "head"),
        P(None, ("groups", "ctx"), "head"),
        P(None, ("groups", "ctx"), "head"),
        P(("groups", "ctx")),
        P(("groups", "ctx"), "head"),
        P(None, ("groups", "ctx"), "head"),
        P("groups"),
    )
    out_specs = (P(("groups", "ctx"), "head"), P(("groups", "ctx"), "head"))
    return jax.shard_map(
        make_local(mesh.shape["ctx"]),
        mesh=mesh,
        in_specs=in_specs,
        out_specs=out_specs,
        check_vma=False,
    )
```

```python
import functools

import jax
import jax.numpy as jnp
from jax import lax
from jax.experimental import pallas as pl
from jax.experimental.pallas import tpu as pltpu
from jax.sharding import PartitionSpec as P

HD = 128
STACK_ROWS = 512


masked_score = -1e30


def widen(per_head):
    return jnp.repeat(per_head, HD, axis=-1)


def attention_kernel(masks, slots, normalize, packed, group_size, kv_heads, ctx_count, query_count, *refs):
    scalar_ref = refs[0]
    q_refs = refs[1 : 1 + query_count]
    part_count = len(masks)
    kv_refs = refs[1 + query_count : 1 + query_count + 2 * part_count]
    rest = refs[1 + query_count + 2 * part_count :]
    if "pos" in masks:
        key_pos_ref, own_pos_ref = rest[0], rest[1]
        rest = rest[2:]
    out_ref = rest[0]
    side_ref = None if normalize or packed else rest[1]
    query_width = kv_heads * group_size * HD
    slot_rows = q_refs[0].shape[0]
    rows = slot_rows * query_count
    scale = 1.0 / jnp.sqrt(jnp.float32(HD))
    stack = max(1, min(group_size, STACK_ROWS // rows))
    visible = []
    if "pos" in masks:
        own_col = own_pos_ref[...]
        if stack > 1:
            own_col = jnp.concatenate([own_col] * stack, axis=0)
    for index, mask in enumerate(masks):
        key_count = kv_refs[2 * index].shape[0]
        shape = (rows * stack, key_count)
        if mask is None:
            visible.append(None)
        elif mask == "cache":
            cols = lax.broadcasted_iota(jnp.int32, shape, 1)
            visible.append(cols < scalar_ref[0])
        elif mask == "causal":
            cols = lax.broadcasted_iota(jnp.int32, shape, 1)
            tokens = lax.broadcasted_iota(jnp.int32, shape, 0)
            if stack > 1:
                tokens = lax.rem(tokens, rows)
            visible.append(cols <= tokens)
        else:
            visible.append(key_pos_ref[...] <= own_col)
    for first in range(0, group_size, stack):
        heads = list(range(first, min(group_size, first + stack)))
        pieces = [q_ref[:, h * HD : (h + 1) * HD] for h in heads for q_ref in q_refs]
        lhs = pieces[0] if len(pieces) == 1 else jnp.concatenate(pieces, axis=0)
        m_rows = lhs.shape[0]
        all_scores = []
        for index in range(part_count):
            raw = lax.dot_general(
                lhs,
                kv_refs[2 * index][...],
                (((1,), (1,)), ((), ())),
                preferred_element_type=jnp.float32,
            )
            if visible[index] is not None:
                raw = jnp.where(visible[index][:m_rows], raw, -jnp.inf)
            all_scores.append(raw)
        peak = jnp.max(all_scores[0], axis=1, keepdims=True)
        for raw in all_scores[1:]:
            peak = jnp.maximum(peak, jnp.max(raw, axis=1, keepdims=True))
        peak = peak * scale
        total = None
        output = None
        for index, raw in enumerate(all_scores):
            weights = jnp.exp(raw * scale - peak)
            part_total = jnp.sum(weights, axis=1, keepdims=True)
            part_output = jnp.dot(
                weights.astype(jnp.bfloat16),
                kv_refs[2 * index + 1][...],
                preferred_element_type=jnp.float32,
            )
            total = part_total if total is None else total + part_total
            output = part_output if output is None else output + part_output
        for slot, h in enumerate(heads):
            rows_of = slice(slot * rows, (slot + 1) * rows)
            if normalize:
                out_ref[:, h * HD : (h + 1) * HD] = (output[rows_of] / total[rows_of]).astype(
                    out_ref.dtype
                )
            elif packed:

                def store(gi, h=h, rows_of=rows_of):
                    head = gi * group_size + h
                    out_ref[:, head * HD : (head + 1) * HD] = output[rows_of]
                    side = query_width + gi * HD
                    out_ref[:, side + h : side + h + 1] = peak[rows_of]
                    side += HD // 2
                    out_ref[:, side + h : side + h + 1] = total[rows_of]

                for gi in range(kv_heads):
                    pl.when(pl.program_id(0) == gi)(functools.partial(store, gi))
            else:
                out_ref[:, h * HD : (h + 1) * HD] = output[rows_of]
                side_ref[:, h : h + 1] = peak[rows_of]
                side_ref[:, HD // 2 + h : HD // 2 + h + 1] = total[rows_of]


def attention(query_slots, parts, normalize, scalars, query_width, pos=None, packed=False):
    slot_rows = query_slots[0].shape[0]
    rows = slot_rows * len(query_slots)
    if len(parts[0]) > 2:
        kv_width = (parts[0][0].shape[1] - query_width) // 2
    else:
        kv_width = parts[0][0].shape[-1]
    kv_heads = kv_width // HD
    group_size = query_width // HD // kv_heads
    group_width = group_size * HD
    masks = tuple(part[1] for part in parts)
    slots = tuple(part[2] if len(part) > 2 else None for part in parts)
    in_specs = [pl.BlockSpec((slot_rows, group_width), lambda g, s: (0, g)) for _ in query_slots]
    operands = list(query_slots)
    for part in parts:
        array = part[0]
        if len(part) > 2:
            first = query_width // HD
            in_specs.append(pl.BlockSpec((array.shape[0], HD), lambda g, s, c=first: (0, c + g)))
            in_specs.append(
                pl.BlockSpec((array.shape[0], HD), lambda g, s, c=first + kv_heads: (0, c + g))
            )
        else:
            key_count = array.shape[1]
            in_specs.append(pl.BlockSpec((pl.Squeezed(), key_count, HD), lambda g, s: (0, 0, g)))
            in_specs.append(pl.BlockSpec((pl.Squeezed(), key_count, HD), lambda g, s: (1, 0, g)))
        operands += [array, array]
    ctx_count = 1
    if pos is not None:
        key_pos = pos[0].reshape(1, -1)
        own_pos = pos[1].reshape(-1, 1)
        in_specs.append(pl.BlockSpec(key_pos.shape, lambda g, s: (0, 0)))
        in_specs.append(pl.BlockSpec(own_pos.shape, lambda g, s: (0, 0)))
        operands += [key_pos, own_pos]
    out_shape = [
        jax.ShapeDtypeStruct((rows, query_width), jnp.bfloat16 if normalize else jnp.float32)
    ]
    out_specs = [pl.BlockSpec((rows, group_width), lambda g, s: (0, g))]
    if packed:
        full = (rows, query_width + kv_heads * HD)
        out_shape = [jax.ShapeDtypeStruct(full, jnp.float32)]
        out_specs = [pl.BlockSpec(full, lambda g, s: (0, 0))]
    elif not normalize:
        out_shape.append(jax.ShapeDtypeStruct((kv_heads, rows, HD), jnp.float32))
        out_specs.append(pl.BlockSpec((pl.Squeezed(), rows, HD), lambda g, s: (g, 0, 0)))
    kernel = functools.partial(
        attention_kernel,
        masks,
        slots,
        normalize,
        packed,
        group_size,
        kv_heads,
        ctx_count,
        len(query_slots),
    )
    return pl.pallas_call(
        kernel,
        grid_spec=pltpu.PrefetchScalarGridSpec(
            num_scalar_prefetch=1,
            grid=(kv_heads,),
            in_specs=in_specs,
            out_specs=out_specs,
        ),
        out_shape=out_shape,
    )(scalars, *operands)


def shifted(value, shift, count):
    return lax.ppermute(value, "ctx", [(j, (j + shift) % count) for j in range(count)])


def make_local(ctx_count):
    def local(q_block, kv_block, anchor_kv, cache_kv, cache_len, query_q, query_kv, query_pos):
        me = lax.axis_index("ctx")
        own_count = query_q.shape[0]
        width = kv_block.shape[2]
        query_width = query_q.shape[1]
        kv_heads = width // HD
        group_size = query_width // HD // kv_heads
        packed = jnp.concatenate([query_q, query_kv[0], query_kv[1]], axis=1)
        query_slots = [packed] + [shifted(packed, k, ctx_count) for k in range(1, ctx_count)]
        anchor_slots = [anchor_kv] + [shifted(anchor_kv, k, ctx_count) for k in range(1, ctx_count)]
        scalars = jnp.stack([cache_len[0], me.astype(jnp.int32)])
        anchor = jnp.concatenate(anchor_slots, axis=1)
        key_columns = [slot[:, query_width:] for slot in query_slots]
        all_query_kv = jnp.stack(
            [
                jnp.concatenate([c[:, :width] for c in key_columns], axis=0),
                jnp.concatenate([c[:, width:] for c in key_columns], axis=0),
            ]
        )
        slot_pos = jnp.concatenate(
            [
                lax.dynamic_slice_in_dim(query_pos, ((me - k) % ctx_count) * own_count, own_count)
                for k in range(ctx_count)
            ]
        )
        own_pos = slot_pos[:own_count]

        (context_packed,) = attention(
            query_slots,
            [(cache_kv, "cache"), (kv_block, None)],
            False,
            scalars,
            query_width,
            packed=True,
        )
        sections = [context_packed[:own_count]]
        for k in range(1, ctx_count):
            rows = slice(k * own_count, (k + 1) * own_count)
            sections.append(shifted(context_packed[rows], -k, ctx_count))
        remote = [
            (
                section[:, :query_width],
                jnp.transpose(section[:, query_width:].reshape(own_count, kv_heads, HD), (1, 0, 2)),
            )
            for section in sections
        ]

        (block_out,) = attention(
            [q_block], [(anchor, None), (kv_block, "causal")], True, scalars, query_width
        )
        local_output, local_side = attention(
            [query_q],
            [(anchor, None), (all_query_kv, "pos")],
            False,
            scalars,
            query_width,
            pos=(slot_pos, own_pos),
        )

        def per_head(side, first):
            picked = side[:, :, first : first + group_size]
            return jnp.transpose(picked, (1, 0, 2)).reshape(own_count, kv_heads * group_size)

        parts = [(local_output, local_side)] + remote
        peaks = [per_head(side, 0) for _, side in parts]
        totals = [per_head(side, HD // 2) for _, side in parts]
        outputs = [output for output, _ in parts]
        top_score = peaks[0]
        for peak in peaks[1:]:
            top_score = jnp.maximum(top_score, peak)
        merged_totals = None
        merged_output = None
        for peak, total, output in zip(peaks, totals, outputs):
            factor = jnp.exp(peak - top_score)
            t = total * factor
            o = output * widen(factor)
            merged_totals = t if merged_totals is None else merged_totals + t
            merged_output = o if merged_output is None else merged_output + o
        query_out = (merged_output / widen(merged_totals)).astype(jnp.bfloat16)
        return (block_out, query_out)

    return local


def solution(mesh):
    in_specs = (
        P(("groups", "ctx"), "head"),
        P(None, ("groups", "ctx"), "head"),
        P(None, ("groups", "ctx"), "head"),
        P(None, ("groups", "ctx"), "head"),
        P(("groups", "ctx")),
        P(("groups", "ctx"), "head"),
        P(None, ("groups", "ctx"), "head"),
        P("groups"),
    )
    out_specs = (P(("groups", "ctx"), "head"), P(("groups", "ctx"), "head"))
    return jax.shard_map(
        make_local(mesh.shape["ctx"]),
        mesh=mesh,
        in_specs=in_specs,
        out_specs=out_specs,
        check_vma=False,
    )
```

```python
import functools

import jax
import jax.numpy as jnp
from jax import lax
from jax.experimental import pallas as pl
from jax.experimental.pallas import tpu as pltpu
from jax.sharding import PartitionSpec as P

HD = 128


masked_score = -1e30


def widen(per_head):
    return jnp.repeat(per_head, HD, axis=-1)


STACK_ROWS = 512
CONTEXT_STACK_ROWS = 256


def attention_kernel(masks, normalize, packed, rows, group_size, kv_heads, stack_rows, *refs):
    length_ref, q_ref = refs[0], refs[1]
    part_count = len(masks)
    kv_refs = refs[2 : 2 + 2 * part_count]
    rest = refs[2 + 2 * part_count :]
    if "pos" in masks:
        key_pos_ref, own_pos_ref = rest[0], rest[1]
        rest = rest[2:]
    out_ref = rest[0]
    side_ref = None if normalize or packed else rest[1]
    query_width = kv_heads * group_size * HD
    scale = 1.0 / jnp.sqrt(jnp.float32(HD))
    stack = max(1, min(group_size, stack_rows // rows))
    visible = []
    for index, mask in enumerate(masks):
        key_count = kv_refs[2 * index].shape[0]
        shape = (rows * stack, key_count)
        if mask is None:
            visible.append(None)
        elif mask == "cache":
            cols = lax.broadcasted_iota(jnp.int32, shape, 1)
            visible.append(cols < length_ref[0])
        elif mask == "causal":
            cols = lax.broadcasted_iota(jnp.int32, shape, 1)
            tokens = lax.broadcasted_iota(jnp.int32, shape, 0)
            if stack > 1:
                tokens = lax.rem(tokens, rows)
            visible.append(cols <= tokens)
        else:
            own = own_pos_ref[...]
            if stack > 1:
                own = jnp.concatenate([own] * stack, axis=0)
            visible.append(key_pos_ref[...] <= own)
    for first in range(0, group_size, stack):
        heads = list(range(first, min(group_size, first + stack)))
        if len(heads) == 1:
            lhs = q_ref[:, first * HD : (first + 1) * HD]
        else:
            lhs = jnp.concatenate([q_ref[:, h * HD : (h + 1) * HD] for h in heads], axis=0)
        m_rows = lhs.shape[0]
        all_scores = []
        for index in range(part_count):
            raw = lax.dot_general(
                lhs,
                kv_refs[2 * index][...],
                (((1,), (1,)), ((), ())),
                preferred_element_type=jnp.float32,
            )
            if visible[index] is not None:
                raw = jnp.where(visible[index][:m_rows], raw, -jnp.inf)
            all_scores.append(raw)
        peak = jnp.max(all_scores[0], axis=1, keepdims=True)
        for raw in all_scores[1:]:
            peak = jnp.maximum(peak, jnp.max(raw, axis=1, keepdims=True))
        peak = peak * scale
        total = None
        output = None
        for index, raw in enumerate(all_scores):
            weights = jnp.exp(raw * scale - peak)
            part_total = jnp.sum(weights, axis=1, keepdims=True)
            part_output = jnp.dot(
                weights.astype(jnp.bfloat16),
                kv_refs[2 * index + 1][...],
                preferred_element_type=jnp.float32,
            )
            total = part_total if total is None else total + part_total
            output = part_output if output is None else output + part_output
        for slot, h in enumerate(heads):
            rows_of = slice(slot * rows, (slot + 1) * rows)
            if normalize:
                out_ref[:, h * HD : (h + 1) * HD] = (output[rows_of] / total[rows_of]).astype(
                    out_ref.dtype
                )
            elif packed:

                def store(gi, h=h, rows_of=rows_of):
                    head = gi * group_size + h
                    out_ref[:, head * HD : (head + 1) * HD] = output[rows_of]
                    side = query_width + gi * HD
                    out_ref[:, side + h : side + h + 1] = peak[rows_of]
                    side += HD // 2
                    out_ref[:, side + h : side + h + 1] = total[rows_of]

                for gi in range(kv_heads):
                    pl.when(pl.program_id(0) == gi)(functools.partial(store, gi))
            else:
                out_ref[:, h * HD : (h + 1) * HD] = output[rows_of]
                side_ref[:, h : h + 1] = peak[rows_of]
                side_ref[:, HD // 2 + h : HD // 2 + h + 1] = total[rows_of]


def attention(
    queries, parts, normalize, length=None, positions=None, packed=False, stack_rows=STACK_ROWS
):
    rows, query_width = queries.shape
    kv_heads = parts[0][0].shape[2] // HD
    group_size = query_width // HD // kv_heads
    group_width = group_size * HD
    if length is None:
        length = jnp.zeros((1,), jnp.int32)
    masks = tuple(mask for _, mask in parts)
    in_specs = [pl.BlockSpec((rows, group_width), lambda g, n: (0, g))]
    operands = [queries]
    for pair, _ in parts:
        key_count = pair.shape[1]
        in_specs.append(pl.BlockSpec((pl.Squeezed(), key_count, HD), lambda g, n: (0, 0, g)))
        in_specs.append(pl.BlockSpec((pl.Squeezed(), key_count, HD), lambda g, n: (1, 0, g)))
        operands += [pair, pair]
    if positions is not None:
        key_pos = positions[0].reshape(1, -1)
        own_pos = positions[1].reshape(-1, 1)
        in_specs.append(pl.BlockSpec(key_pos.shape, lambda g, n: (0, 0)))
        in_specs.append(pl.BlockSpec(own_pos.shape, lambda g, n: (0, 0)))
        operands += [key_pos, own_pos]
    out_shape = [
        jax.ShapeDtypeStruct((rows, query_width), jnp.bfloat16 if normalize else jnp.float32)
    ]
    out_specs = [pl.BlockSpec((rows, group_width), lambda g, n: (0, g))]
    if packed:
        full = (rows, query_width + kv_heads * HD)
        out_shape = [jax.ShapeDtypeStruct(full, jnp.float32)]
        out_specs = [pl.BlockSpec(full, lambda g, n: (0, 0))]
    elif not normalize:
        out_shape.append(jax.ShapeDtypeStruct((kv_heads, rows, HD), jnp.float32))
        out_specs.append(pl.BlockSpec((pl.Squeezed(), rows, HD), lambda g, n: (g, 0, 0)))
    return pl.pallas_call(
        functools.partial(
            attention_kernel, masks, normalize, packed, rows, group_size, kv_heads, stack_rows
        ),
        grid_spec=pltpu.PrefetchScalarGridSpec(
            num_scalar_prefetch=1,
            grid=(kv_heads,),
            in_specs=in_specs,
            out_specs=out_specs,
        ),
        out_shape=out_shape,
    )(length, *operands)


def shifted(value, shift, count):
    return lax.ppermute(value, "ctx", [(j, (j + shift) % count) for j in range(count)])


def make_local(ctx_count):
    def local(q_block, kv_block, anchor_kv, cache_kv, cache_len, query_q, query_kv, query_pos):
        me = lax.axis_index("ctx")
        own_count = query_q.shape[0]
        width = kv_block.shape[2]
        query_width = query_q.shape[1]
        kv_heads = width // HD
        group_size = query_width // HD // kv_heads
        packed = jnp.concatenate([query_q.reshape(-1), query_kv.reshape(-1)])
        query_slots = [packed] + [shifted(packed, k, ctx_count) for k in range(1, ctx_count)]
        anchor_slots = [anchor_kv] + [shifted(anchor_kv, k, ctx_count) for k in range(1, ctx_count)]
        split = own_count * query_width
        all_queries = jnp.concatenate(
            [slot[:split].reshape(own_count, query_width) for slot in query_slots], axis=0
        )
        all_query_kv = jnp.concatenate(
            [slot[split:].reshape(2, own_count, width) for slot in query_slots], axis=1
        )
        anchor = jnp.concatenate(anchor_slots, axis=1)
        slot_pos = jnp.concatenate(
            [
                lax.dynamic_slice_in_dim(query_pos, ((me - k) % ctx_count) * own_count, own_count)
                for k in range(ctx_count)
            ]
        )
        own_pos = slot_pos[:own_count]

        (context_packed,) = attention(
            all_queries,
            [(cache_kv, "cache"), (kv_block, None)],
            False,
            length=cache_len,
            packed=True,
            stack_rows=CONTEXT_STACK_ROWS,
        )
        sections = [context_packed[:own_count]]
        for k in range(1, ctx_count):
            rows = slice(k * own_count, (k + 1) * own_count)
            sections.append(shifted(context_packed[rows], -k, ctx_count))
        remote = [
            (
                section[:, :query_width],
                jnp.transpose(section[:, query_width:].reshape(own_count, kv_heads, HD), (1, 0, 2)),
            )
            for section in sections
        ]

        (block_out,) = attention(q_block, [(anchor, None), (kv_block, "causal")], True)
        local_output, local_side = attention(
            query_q,
            [(anchor, None), (all_query_kv, "pos")],
            False,
            positions=(slot_pos, own_pos),
        )

        def per_head(side, first):
            picked = side[:, :, first : first + group_size]
            return jnp.transpose(picked, (1, 0, 2)).reshape(own_count, kv_heads * group_size)

        parts = [(local_output, local_side)] + remote
        peaks = [per_head(side, 0) for _, side in parts]
        totals = [per_head(side, HD // 2) for _, side in parts]
        outputs = [output for output, _ in parts]
        top_score = peaks[0]
        for peak in peaks[1:]:
            top_score = jnp.maximum(top_score, peak)
        merged_totals = None
        merged_output = None
        for peak, total, output in zip(peaks, totals, outputs):
            factor = jnp.exp(peak - top_score)
            t = total * factor
            o = output * widen(factor)
            merged_totals = t if merged_totals is None else merged_totals + t
            merged_output = o if merged_output is None else merged_output + o
        query_out = (merged_output / widen(merged_totals)).astype(jnp.bfloat16)
        return (block_out, query_out)

    return local


def solution(mesh):
    in_specs = (
        P(("groups", "ctx"), "head"),
        P(None, ("groups", "ctx"), "head"),
        P(None, ("groups", "ctx"), "head"),
        P(None, ("groups", "ctx"), "head"),
        P(("groups", "ctx")),
        P(("groups", "ctx"), "head"),
        P(None, ("groups", "ctx"), "head"),
        P("groups"),
    )
    out_specs = (P(("groups", "ctx"), "head"), P(("groups", "ctx"), "head"))
    return jax.shard_map(
        make_local(mesh.shape["ctx"]),
        mesh=mesh,
        in_specs=in_specs,
        out_specs=out_specs,
        check_vma=False,
    )
```

```python
import functools

import jax
import jax.numpy as jnp
from jax import lax
from jax.experimental import pallas as pl
from jax.experimental.pallas import tpu as pltpu
from jax.sharding import PartitionSpec as P

HD = 128


masked_score = -1e30


def widen(per_head):
    return jnp.repeat(per_head, HD, axis=-1)


STACK_ROWS = 512
CONTEXT_STACK_ROWS = 256


def attention_kernel(
    masks, normalize, packed, rows, group_size, kv_heads, stack_rows, merge_count, *refs
):
    length_ref, q_ref = refs[0], refs[1]
    part_count = len(masks)
    kv_refs = refs[2 : 2 + 2 * part_count]
    rest = refs[2 + 2 * part_count :]
    if "pos" in masks:
        key_pos_ref, own_pos_ref = rest[0], rest[1]
        rest = rest[2:]
    section_refs = rest[: 2 * merge_count]
    rest = rest[2 * merge_count :]
    out_ref = rest[0]
    side_ref = None if normalize or packed or merge_count else rest[1]
    query_width = kv_heads * group_size * HD
    scale = 1.0 / jnp.sqrt(jnp.float32(HD))
    stack = max(1, min(group_size, stack_rows // rows))
    visible = []
    for index, mask in enumerate(masks):
        key_count = kv_refs[2 * index].shape[0]
        shape = (rows * stack, key_count)
        if mask is None:
            visible.append(None)
        elif mask == "cache":
            cols = lax.broadcasted_iota(jnp.int32, shape, 1)
            visible.append(cols < length_ref[0])
        elif mask == "causal":
            cols = lax.broadcasted_iota(jnp.int32, shape, 1)
            tokens = lax.broadcasted_iota(jnp.int32, shape, 0)
            if stack > 1:
                tokens = lax.rem(tokens, rows)
            visible.append(cols <= tokens)
        else:
            own = own_pos_ref[...]
            if stack > 1:
                own = jnp.concatenate([own] * stack, axis=0)
            visible.append(key_pos_ref[...] <= own)
    for first in range(0, group_size, stack):
        heads = list(range(first, min(group_size, first + stack)))
        if len(heads) == 1:
            lhs = q_ref[:, first * HD : (first + 1) * HD]
        else:
            lhs = jnp.concatenate([q_ref[:, h * HD : (h + 1) * HD] for h in heads], axis=0)
        m_rows = lhs.shape[0]
        all_scores = []
        for index in range(part_count):
            raw = lax.dot_general(
                lhs,
                kv_refs[2 * index][...],
                (((1,), (1,)), ((), ())),
                preferred_element_type=jnp.float32,
            )
            if visible[index] is not None:
                raw = jnp.where(visible[index][:m_rows], raw, -jnp.inf)
            all_scores.append(raw)
        peak = jnp.max(all_scores[0], axis=1, keepdims=True)
        for raw in all_scores[1:]:
            peak = jnp.maximum(peak, jnp.max(raw, axis=1, keepdims=True))
        peak = peak * scale
        total = None
        output = None
        for index, raw in enumerate(all_scores):
            weights = jnp.exp(raw * scale - peak)
            part_total = jnp.sum(weights, axis=1, keepdims=True)
            part_output = jnp.dot(
                weights.astype(jnp.bfloat16),
                kv_refs[2 * index + 1][...],
                preferred_element_type=jnp.float32,
            )
            total = part_total if total is None else total + part_total
            output = part_output if output is None else output + part_output
        for slot, h in enumerate(heads):
            rows_of = slice(slot * rows, (slot + 1) * rows)
            if merge_count:
                peaks = [peak[rows_of]]
                totals = [total[rows_of]]
                outputs = [output[rows_of]]
                for index in range(merge_count):
                    section_o, section_side = section_refs[2 * index], section_refs[2 * index + 1]
                    peaks.append(section_side[:, h : h + 1])
                    totals.append(section_side[:, HD // 2 + h : HD // 2 + h + 1])
                    outputs.append(section_o[:, h * HD : (h + 1) * HD])
                top = peaks[0]
                for value in peaks[1:]:
                    top = jnp.maximum(top, value)
                merged_total = None
                merged_output = None
                for value, part_total, part_output in zip(peaks, totals, outputs):
                    factor = jnp.exp(value - top)
                    t = part_total * factor
                    o = part_output * factor
                    merged_total = t if merged_total is None else merged_total + t
                    merged_output = o if merged_output is None else merged_output + o
                out_ref[:, h * HD : (h + 1) * HD] = (merged_output / merged_total).astype(
                    out_ref.dtype
                )
            elif normalize:
                out_ref[:, h * HD : (h + 1) * HD] = (output[rows_of] / total[rows_of]).astype(
                    out_ref.dtype
                )
            elif packed:

                def store(gi, h=h, rows_of=rows_of):
                    head = gi * group_size + h
                    out_ref[:, head * HD : (head + 1) * HD] = output[rows_of]
                    side = query_width + gi * HD
                    out_ref[:, side + h : side + h + 1] = peak[rows_of]
                    side += HD // 2
                    out_ref[:, side + h : side + h + 1] = total[rows_of]

                for gi in range(kv_heads):
                    pl.when(pl.program_id(0) == gi)(functools.partial(store, gi))
            else:
                out_ref[:, h * HD : (h + 1) * HD] = output[rows_of]
                side_ref[:, h : h + 1] = peak[rows_of]
                side_ref[:, HD // 2 + h : HD // 2 + h + 1] = total[rows_of]


def attention(
    queries,
    parts,
    normalize,
    length=None,
    positions=None,
    packed=False,
    stack_rows=STACK_ROWS,
    sections=(),
):
    rows, query_width = queries.shape
    kv_heads = parts[0][0].shape[2] // HD
    group_size = query_width // HD // kv_heads
    group_width = group_size * HD
    if length is None:
        length = jnp.zeros((1,), jnp.int32)
    masks = tuple(mask for _, mask in parts)
    in_specs = [pl.BlockSpec((rows, group_width), lambda g, n: (0, g))]
    operands = [queries]
    for pair, _ in parts:
        key_count = pair.shape[1]
        in_specs.append(pl.BlockSpec((pl.Squeezed(), key_count, HD), lambda g, n: (0, 0, g)))
        in_specs.append(pl.BlockSpec((pl.Squeezed(), key_count, HD), lambda g, n: (1, 0, g)))
        operands += [pair, pair]
    if positions is not None:
        key_pos = positions[0].reshape(1, -1)
        own_pos = positions[1].reshape(-1, 1)
        in_specs.append(pl.BlockSpec(key_pos.shape, lambda g, n: (0, 0)))
        in_specs.append(pl.BlockSpec(own_pos.shape, lambda g, n: (0, 0)))
        operands += [key_pos, own_pos]
    for section in sections:
        side_block = query_width // HD
        in_specs.append(pl.BlockSpec((rows, group_width), lambda g, n: (0, g)))
        in_specs.append(pl.BlockSpec((rows, HD), lambda g, n, c=side_block: (0, c + g)))
        operands += [section, section]
    if sections:
        normalize = True
    out_shape = [
        jax.ShapeDtypeStruct((rows, query_width), jnp.bfloat16 if normalize else jnp.float32)
    ]
    out_specs = [pl.BlockSpec((rows, group_width), lambda g, n: (0, g))]
    if packed:
        full = (rows, query_width + kv_heads * HD)
        out_shape = [jax.ShapeDtypeStruct(full, jnp.float32)]
        out_specs = [pl.BlockSpec(full, lambda g, n: (0, 0))]
    elif not normalize:
        out_shape.append(jax.ShapeDtypeStruct((kv_heads, rows, HD), jnp.float32))
        out_specs.append(pl.BlockSpec((pl.Squeezed(), rows, HD), lambda g, n: (g, 0, 0)))
    return pl.pallas_call(
        functools.partial(
            attention_kernel,
            masks,
            normalize,
            packed,
            rows,
            group_size,
            kv_heads,
            stack_rows,
            len(sections),
        ),
        grid_spec=pltpu.PrefetchScalarGridSpec(
            num_scalar_prefetch=1,
            grid=(kv_heads,),
            in_specs=in_specs,
            out_specs=out_specs,
        ),
        out_shape=out_shape,
    )(length, *operands)


def shifted(value, shift, count):
    return lax.ppermute(value, "ctx", [(j, (j + shift) % count) for j in range(count)])


def make_local(ctx_count):
    def local(q_block, kv_block, anchor_kv, cache_kv, cache_len, query_q, query_kv, query_pos):
        me = lax.axis_index("ctx")
        own_count = query_q.shape[0]
        width = kv_block.shape[2]
        query_width = query_q.shape[1]
        kv_heads = width // HD
        group_size = query_width // HD // kv_heads
        packed = jnp.concatenate([query_q.reshape(-1), query_kv.reshape(-1)])
        query_slots = [packed] + [shifted(packed, k, ctx_count) for k in range(1, ctx_count)]
        anchor_slots = [anchor_kv] + [shifted(anchor_kv, k, ctx_count) for k in range(1, ctx_count)]
        split = own_count * query_width
        all_queries = jnp.concatenate(
            [slot[:split].reshape(own_count, query_width) for slot in query_slots], axis=0
        )
        all_query_kv = jnp.concatenate(
            [slot[split:].reshape(2, own_count, width) for slot in query_slots], axis=1
        )
        anchor = jnp.concatenate(anchor_slots, axis=1)
        slot_pos = jnp.concatenate(
            [
                lax.dynamic_slice_in_dim(query_pos, ((me - k) % ctx_count) * own_count, own_count)
                for k in range(ctx_count)
            ]
        )
        own_pos = slot_pos[:own_count]

        (context_packed,) = attention(
            all_queries,
            [(cache_kv, "cache"), (kv_block, None)],
            False,
            length=cache_len,
            packed=True,
            stack_rows=CONTEXT_STACK_ROWS,
        )
        sections = [context_packed[:own_count]]
        for k in range(1, ctx_count):
            rows = slice(k * own_count, (k + 1) * own_count)
            sections.append(shifted(context_packed[rows], -k, ctx_count))
        (block_out,) = attention(q_block, [(anchor, None), (kv_block, "causal")], True)
        (query_out,) = attention(
            query_q,
            [(anchor, None), (all_query_kv, "pos")],
            False,
            positions=(slot_pos, own_pos),
            sections=sections,
        )
        return (block_out, query_out)

    return local


def solution(mesh):
    in_specs = (
        P(("groups", "ctx"), "head"),
        P(None, ("groups", "ctx"), "head"),
        P(None, ("groups", "ctx"), "head"),
        P(None, ("groups", "ctx"), "head"),
        P(("groups", "ctx")),
        P(("groups", "ctx"), "head"),
        P(None, ("groups", "ctx"), "head"),
        P("groups"),
    )
    out_specs = (P(("groups", "ctx"), "head"), P(("groups", "ctx"), "head"))
    return jax.shard_map(
        make_local(mesh.shape["ctx"]),
        mesh=mesh,
        in_specs=in_specs,
        out_specs=out_specs,
        check_vma=False,
    )
```

```python
import functools

import jax
import jax.numpy as jnp
from jax import lax
from jax.experimental import pallas as pl
from jax.experimental.pallas import tpu as pltpu
from jax.sharding import PartitionSpec as P

HD = 128


masked_score = -1e30


def widen(per_head):
    return jnp.repeat(per_head, HD, axis=-1)


STACK_ROWS = 512
CONTEXT_STACK_ROWS = 256


def attention_kernel(
    masks, normalize, packed, rows, group_size, kv_heads, stack_rows, merge_count, *refs
):
    length_ref, q_ref = refs[0], refs[1]
    part_count = len(masks)
    kv_refs = refs[2 : 2 + 2 * part_count]
    rest = refs[2 + 2 * part_count :]
    if "pos" in masks:
        key_pos_ref, own_pos_ref = rest[0], rest[1]
        rest = rest[2:]
    section_refs = rest[: 2 * merge_count]
    rest = rest[2 * merge_count :]
    out_ref = rest[0]
    side_ref = None if normalize or packed or merge_count else rest[1]
    query_width = kv_heads * group_size * HD
    scale = 1.0 / jnp.sqrt(jnp.float32(HD))
    stack = max(1, min(group_size, stack_rows // rows))
    visible = []
    for index, mask in enumerate(masks):
        key_count = kv_refs[2 * index].shape[0]
        shape = (rows * stack, key_count)
        if mask is None:
            visible.append(None)
        elif mask == "cache":
            cols = lax.broadcasted_iota(jnp.int32, shape, 1)
            visible.append(cols < length_ref[0])
        elif mask == "causal":
            cols = lax.broadcasted_iota(jnp.int32, shape, 1)
            tokens = lax.broadcasted_iota(jnp.int32, shape, 0)
            if stack > 1:
                tokens = lax.rem(tokens, rows)
            visible.append(cols <= tokens)
        else:
            own = own_pos_ref[...]
            if stack > 1:
                own = jnp.concatenate([own] * stack, axis=0)
            visible.append(key_pos_ref[...] <= own)
    for first in range(0, group_size, stack):
        heads = list(range(first, min(group_size, first + stack)))
        if len(heads) == 1:
            lhs = q_ref[:, first * HD : (first + 1) * HD]
        else:
            lhs = jnp.concatenate([q_ref[:, h * HD : (h + 1) * HD] for h in heads], axis=0)
        m_rows = lhs.shape[0]
        all_scores = []
        for index in range(part_count):
            raw = lax.dot_general(
                lhs,
                kv_refs[2 * index][...],
                (((1,), (1,)), ((), ())),
                preferred_element_type=jnp.float32,
            )
            if visible[index] is not None:
                raw = jnp.where(visible[index][:m_rows], raw, -jnp.inf)
            all_scores.append(raw)
        peak = jnp.max(all_scores[0], axis=1, keepdims=True)
        for raw in all_scores[1:]:
            peak = jnp.maximum(peak, jnp.max(raw, axis=1, keepdims=True))
        peak = peak * scale
        total = None
        output = None
        for index, raw in enumerate(all_scores):
            weights = jnp.exp(raw * scale - peak)
            part_total = jnp.sum(weights, axis=1, keepdims=True)
            part_output = jnp.dot(
                weights.astype(jnp.bfloat16),
                kv_refs[2 * index + 1][...],
                preferred_element_type=jnp.float32,
            )
            total = part_total if total is None else total + part_total
            output = part_output if output is None else output + part_output
        for slot, h in enumerate(heads):
            rows_of = slice(slot * rows, (slot + 1) * rows)
            if merge_count:
                peaks = [peak[rows_of]]
                totals = [total[rows_of]]
                outputs = [output[rows_of]]
                for index in range(merge_count):
                    section_o, section_side = section_refs[2 * index], section_refs[2 * index + 1]
                    peaks.append(section_side[:, h : h + 1])
                    totals.append(section_side[:, HD // 2 + h : HD // 2 + h + 1])
                    outputs.append(section_o[:, h * HD : (h + 1) * HD])
                top = peaks[0]
                for value in peaks[1:]:
                    top = jnp.maximum(top, value)
                merged_total = None
                merged_output = None
                for value, part_total, part_output in zip(peaks, totals, outputs):
                    factor = jnp.exp(value - top)
                    t = part_total * factor
                    o = part_output * factor
                    merged_total = t if merged_total is None else merged_total + t
                    merged_output = o if merged_output is None else merged_output + o
                out_ref[:, h * HD : (h + 1) * HD] = (merged_output / merged_total).astype(
                    out_ref.dtype
                )
            elif normalize:
                out_ref[:, h * HD : (h + 1) * HD] = (output[rows_of] / total[rows_of]).astype(
                    out_ref.dtype
                )
            elif packed:

                def store(gi, h=h, rows_of=rows_of):
                    head = gi * group_size + h
                    out_ref[:, head * HD : (head + 1) * HD] = output[rows_of]
                    side = query_width + gi * HD
                    out_ref[:, side + h : side + h + 1] = peak[rows_of]
                    side += HD // 2
                    out_ref[:, side + h : side + h + 1] = total[rows_of]

                for gi in range(kv_heads):
                    pl.when(pl.program_id(0) == gi)(functools.partial(store, gi))
            else:
                out_ref[:, h * HD : (h + 1) * HD] = output[rows_of]
                side_ref[:, h : h + 1] = peak[rows_of]
                side_ref[:, HD // 2 + h : HD // 2 + h + 1] = total[rows_of]


def attention(
    queries,
    parts,
    normalize,
    length=None,
    positions=None,
    packed=False,
    stack_rows=STACK_ROWS,
    sections=(),
):
    rows, query_width = queries.shape
    kv_heads = parts[0][0].shape[2] // HD
    group_size = query_width // HD // kv_heads
    group_width = group_size * HD
    if length is None:
        length = jnp.zeros((1,), jnp.int32)
    masks = tuple(mask for _, mask in parts)
    in_specs = [pl.BlockSpec((rows, group_width), lambda g, n: (0, g))]
    operands = [queries]
    for pair, _ in parts:
        key_count = pair.shape[1]
        in_specs.append(pl.BlockSpec((pl.Squeezed(), key_count, HD), lambda g, n: (0, 0, g)))
        in_specs.append(pl.BlockSpec((pl.Squeezed(), key_count, HD), lambda g, n: (1, 0, g)))
        operands += [pair, pair]
    if positions is not None:
        key_pos = positions[0].reshape(1, -1)
        own_pos = positions[1].reshape(-1, 1)
        in_specs.append(pl.BlockSpec(key_pos.shape, lambda g, n: (0, 0)))
        in_specs.append(pl.BlockSpec(own_pos.shape, lambda g, n: (0, 0)))
        operands += [key_pos, own_pos]
    for section in sections:
        side_block = query_width // HD
        in_specs.append(pl.BlockSpec((rows, group_width), lambda g, n: (0, g)))
        in_specs.append(pl.BlockSpec((rows, HD), lambda g, n, c=side_block: (0, c + g)))
        operands += [section, section]
    if sections:
        normalize = True
    out_shape = [
        jax.ShapeDtypeStruct((rows, query_width), jnp.bfloat16 if normalize else jnp.float32)
    ]
    out_specs = [pl.BlockSpec((rows, group_width), lambda g, n: (0, g))]
    if packed:
        full = (rows, query_width + kv_heads * HD)
        out_shape = [jax.ShapeDtypeStruct(full, jnp.float32)]
        out_specs = [pl.BlockSpec(full, lambda g, n: (0, 0))]
    elif not normalize:
        out_shape.append(jax.ShapeDtypeStruct((kv_heads, rows, HD), jnp.float32))
        out_specs.append(pl.BlockSpec((pl.Squeezed(), rows, HD), lambda g, n: (g, 0, 0)))
    return pl.pallas_call(
        functools.partial(
            attention_kernel,
            masks,
            normalize,
            packed,
            rows,
            group_size,
            kv_heads,
            stack_rows,
            len(sections),
        ),
        grid_spec=pltpu.PrefetchScalarGridSpec(
            num_scalar_prefetch=1,
            grid=(kv_heads,),
            in_specs=in_specs,
            out_specs=out_specs,
        ),
        out_shape=out_shape,
    )(length, *operands)


def shifted(value, shift, count):
    return lax.ppermute(value, "ctx", [(j, (j + shift) % count) for j in range(count)])


def make_local(ctx_count):
    def local(q_block, kv_block, anchor_kv, cache_kv, cache_len, query_q, query_kv, query_pos):
        me = lax.axis_index("ctx")
        own_count = query_q.shape[0]
        width = kv_block.shape[2]
        query_width = query_q.shape[1]
        kv_heads = width // HD
        group_size = query_width // HD // kv_heads
        packed = jnp.concatenate([query_q.reshape(-1), query_kv.reshape(-1)])
        query_slots = [packed] + [shifted(packed, k, ctx_count) for k in range(1, ctx_count)]
        split = own_count * query_width
        all_queries = jnp.concatenate(
            [slot[:split].reshape(own_count, query_width) for slot in query_slots], axis=0
        )
        anchor_kv, all_queries = lax.optimization_barrier((anchor_kv, all_queries))
        anchor_slots = [anchor_kv] + [shifted(anchor_kv, k, ctx_count) for k in range(1, ctx_count)]
        all_query_kv = jnp.concatenate(
            [slot[split:].reshape(2, own_count, width) for slot in query_slots], axis=1
        )
        anchor = jnp.concatenate(anchor_slots, axis=1)
        slot_pos = jnp.concatenate(
            [
                lax.dynamic_slice_in_dim(query_pos, ((me - k) % ctx_count) * own_count, own_count)
                for k in range(ctx_count)
            ]
        )
        own_pos = slot_pos[:own_count]

        (context_packed,) = attention(
            all_queries,
            [(cache_kv, "cache"), (kv_block, None)],
            False,
            length=cache_len,
            packed=True,
            stack_rows=CONTEXT_STACK_ROWS,
        )
        sections = [context_packed[:own_count]]
        for k in range(1, ctx_count):
            rows = slice(k * own_count, (k + 1) * own_count)
            sections.append(shifted(context_packed[rows], -k, ctx_count))
        (block_out,) = attention(q_block, [(anchor, None), (kv_block, "causal")], True)
        (query_out,) = attention(
            query_q,
            [(anchor, None), (all_query_kv, "pos")],
            False,
            positions=(slot_pos, own_pos),
            sections=sections,
        )
        return (block_out, query_out)

    return local


def solution(mesh):
    in_specs = (
        P(("groups", "ctx"), "head"),
        P(None, ("groups", "ctx"), "head"),
        P(None, ("groups", "ctx"), "head"),
        P(None, ("groups", "ctx"), "head"),
        P(("groups", "ctx")),
        P(("groups", "ctx"), "head"),
        P(None, ("groups", "ctx"), "head"),
        P("groups"),
    )
    out_specs = (P(("groups", "ctx"), "head"), P(("groups", "ctx"), "head"))
    return jax.shard_map(
        make_local(mesh.shape["ctx"]),
        mesh=mesh,
        in_specs=in_specs,
        out_specs=out_specs,
        check_vma=False,
    )
```

```python
import functools

import jax
import jax.numpy as jnp
from jax import lax
from jax.experimental import pallas as pl
from jax.experimental.pallas import tpu as pltpu
from jax.sharding import PartitionSpec as P

HD = 128


masked_score = -1e30


def widen(per_head):
    return jnp.repeat(per_head, HD, axis=-1)


STACK_ROWS = 512
CONTEXT_STACK_ROWS = 256


def attention_kernel(
    masks, normalize, packed, rows, group_size, kv_heads, stack_rows, merge_count, *refs
):
    length_ref, q_ref = refs[0], refs[1]
    part_count = len(masks)
    kv_refs = refs[2 : 2 + 2 * part_count]
    rest = refs[2 + 2 * part_count :]
    if "pos" in masks:
        key_pos_ref, own_pos_ref = rest[0], rest[1]
        rest = rest[2:]
    section_refs = rest[: 2 * merge_count]
    rest = rest[2 * merge_count :]
    out_ref = rest[0]
    side_ref = None if normalize or packed or merge_count else rest[1]
    query_width = kv_heads * group_size * HD
    scale = 1.0 / jnp.sqrt(jnp.float32(HD))
    stack = max(1, min(group_size, stack_rows // rows))
    visible = []
    for index, mask in enumerate(masks):
        key_count = kv_refs[2 * index].shape[0]
        shape = (rows * stack, key_count)
        if mask is None:
            visible.append(None)
        elif mask == "cache":
            cols = lax.broadcasted_iota(jnp.int32, shape, 1)
            visible.append(cols < length_ref[0])
        elif mask == "causal":
            cols = lax.broadcasted_iota(jnp.int32, shape, 1)
            tokens = lax.broadcasted_iota(jnp.int32, shape, 0)
            if stack > 1:
                tokens = lax.rem(tokens, rows)
            visible.append(cols <= tokens)
        else:
            own = own_pos_ref[...]
            if stack > 1:
                own = jnp.concatenate([own] * stack, axis=0)
            visible.append(key_pos_ref[...] <= own)
    for first in range(0, group_size, stack):
        heads = list(range(first, min(group_size, first + stack)))
        if len(heads) == 1:
            lhs = q_ref[:, first * HD : (first + 1) * HD]
        else:
            lhs = jnp.concatenate([q_ref[:, h * HD : (h + 1) * HD] for h in heads], axis=0)
        m_rows = lhs.shape[0]
        all_scores = []
        for index in range(part_count):
            raw = lax.dot_general(
                lhs,
                kv_refs[2 * index][...],
                (((1,), (1,)), ((), ())),
                preferred_element_type=jnp.float32,
            )
            if visible[index] is not None:
                raw = jnp.where(visible[index][:m_rows], raw, -jnp.inf)
            all_scores.append(raw)
        peak = jnp.max(all_scores[0], axis=1, keepdims=True)
        for raw in all_scores[1:]:
            peak = jnp.maximum(peak, jnp.max(raw, axis=1, keepdims=True))
        peak = peak * scale
        total = None
        output = None
        for index, raw in enumerate(all_scores):
            weights = jnp.exp(raw * scale - peak)
            part_total = jnp.sum(weights, axis=1, keepdims=True)
            part_output = jnp.dot(
                weights.astype(jnp.bfloat16),
                kv_refs[2 * index + 1][...],
                preferred_element_type=jnp.float32,
            )
            total = part_total if total is None else total + part_total
            output = part_output if output is None else output + part_output
        for slot, h in enumerate(heads):
            rows_of = slice(slot * rows, (slot + 1) * rows)
            if merge_count:
                peaks = [peak[rows_of]]
                totals = [total[rows_of]]
                outputs = [output[rows_of]]
                for index in range(merge_count):
                    section_o, section_side = section_refs[2 * index], section_refs[2 * index + 1]
                    peaks.append(section_side[:, h : h + 1])
                    totals.append(section_side[:, HD // 2 + h : HD // 2 + h + 1])
                    outputs.append(section_o[:, h * HD : (h + 1) * HD])
                top = peaks[0]
                for value in peaks[1:]:
                    top = jnp.maximum(top, value)
                merged_total = None
                merged_output = None
                for value, part_total, part_output in zip(peaks, totals, outputs):
                    factor = jnp.exp(value - top)
                    t = part_total * factor
                    o = part_output * factor
                    merged_total = t if merged_total is None else merged_total + t
                    merged_output = o if merged_output is None else merged_output + o
                out_ref[:, h * HD : (h + 1) * HD] = (merged_output / merged_total).astype(
                    out_ref.dtype
                )
            elif normalize:
                out_ref[:, h * HD : (h + 1) * HD] = (output[rows_of] / total[rows_of]).astype(
                    out_ref.dtype
                )
            elif packed:

                def store(gi, h=h, rows_of=rows_of):
                    head = gi * group_size + h
                    out_ref[:, head * HD : (head + 1) * HD] = output[rows_of]
                    side = query_width + gi * HD
                    out_ref[:, side + h : side + h + 1] = peak[rows_of]
                    side += HD // 2
                    out_ref[:, side + h : side + h + 1] = total[rows_of]

                for gi in range(kv_heads):
                    pl.when(pl.program_id(0) == gi)(functools.partial(store, gi))
            else:
                out_ref[:, h * HD : (h + 1) * HD] = output[rows_of]
                side_ref[:, h : h + 1] = peak[rows_of]
                side_ref[:, HD // 2 + h : HD // 2 + h + 1] = total[rows_of]


def attention(
    queries,
    parts,
    normalize,
    length=None,
    positions=None,
    packed=False,
    stack_rows=STACK_ROWS,
    sections=(),
):
    rows, query_width = queries.shape
    kv_heads = parts[0][0].shape[2] // HD
    group_size = query_width // HD // kv_heads
    group_width = group_size * HD
    if length is None:
        length = jnp.zeros((1,), jnp.int32)
    masks = tuple(mask for _, mask in parts)
    in_specs = [pl.BlockSpec((rows, group_width), lambda g, n: (0, g))]
    operands = [queries]
    for pair, _ in parts:
        key_count = pair.shape[1]
        in_specs.append(pl.BlockSpec((pl.Squeezed(), key_count, HD), lambda g, n: (0, 0, g)))
        in_specs.append(pl.BlockSpec((pl.Squeezed(), key_count, HD), lambda g, n: (1, 0, g)))
        operands += [pair, pair]
    if positions is not None:
        key_pos = positions[0].reshape(1, -1)
        own_pos = positions[1].reshape(-1, 1)
        in_specs.append(pl.BlockSpec(key_pos.shape, lambda g, n: (0, 0)))
        in_specs.append(pl.BlockSpec(own_pos.shape, lambda g, n: (0, 0)))
        operands += [key_pos, own_pos]
    for section in sections:
        side_block = query_width // HD
        in_specs.append(pl.BlockSpec((rows, group_width), lambda g, n: (0, g)))
        in_specs.append(pl.BlockSpec((rows, HD), lambda g, n, c=side_block: (0, c + g)))
        operands += [section, section]
    if sections:
        normalize = True
    out_shape = [
        jax.ShapeDtypeStruct((rows, query_width), jnp.bfloat16 if normalize else jnp.float32)
    ]
    out_specs = [pl.BlockSpec((rows, group_width), lambda g, n: (0, g))]
    if packed:
        full = (rows, query_width + kv_heads * HD)
        out_shape = [jax.ShapeDtypeStruct(full, jnp.float32)]
        out_specs = [pl.BlockSpec(full, lambda g, n: (0, 0))]
    elif not normalize:
        out_shape.append(jax.ShapeDtypeStruct((kv_heads, rows, HD), jnp.float32))
        out_specs.append(pl.BlockSpec((pl.Squeezed(), rows, HD), lambda g, n: (g, 0, 0)))
    return pl.pallas_call(
        functools.partial(
            attention_kernel,
            masks,
            normalize,
            packed,
            rows,
            group_size,
            kv_heads,
            stack_rows,
            len(sections),
        ),
        grid_spec=pltpu.PrefetchScalarGridSpec(
            num_scalar_prefetch=1,
            grid=(kv_heads,),
            in_specs=in_specs,
            out_specs=out_specs,
        ),
        out_shape=out_shape,
    )(length, *operands)


def shifted(value, shift, count):
    return lax.ppermute(value, "ctx", [(j, (j + shift) % count) for j in range(count)])


def make_local(ctx_count):
    def local(q_block, kv_block, anchor_kv, cache_kv, cache_len, query_q, query_kv, query_pos):
        me = lax.axis_index("ctx")
        own_count = query_q.shape[0]
        width = kv_block.shape[2]
        query_width = query_q.shape[1]
        kv_heads = width // HD
        group_size = query_width // HD // kv_heads
        packed = jnp.concatenate([query_q, query_kv[0], query_kv[1]], axis=1)
        query_slots = [packed] + [shifted(packed, k, ctx_count) for k in range(1, ctx_count)]
        anchor_slots = [anchor_kv] + [shifted(anchor_kv, k, ctx_count) for k in range(1, ctx_count)]
        all_rows = jnp.concatenate(query_slots, axis=0)
        all_queries = all_rows[:, :query_width]
        all_query_kv = jnp.stack(
            [
                all_rows[:, query_width : query_width + width],
                all_rows[:, query_width + width :],
            ]
        )
        anchor = jnp.concatenate(anchor_slots, axis=1)
        slot_pos = jnp.concatenate(
            [
                lax.dynamic_slice_in_dim(query_pos, ((me - k) % ctx_count) * own_count, own_count)
                for k in range(ctx_count)
            ]
        )
        own_pos = slot_pos[:own_count]

        (context_packed,) = attention(
            all_queries,
            [(cache_kv, "cache"), (kv_block, None)],
            False,
            length=cache_len,
            packed=True,
            stack_rows=CONTEXT_STACK_ROWS,
        )
        sections = [context_packed[:own_count]]
        for k in range(1, ctx_count):
            rows = slice(k * own_count, (k + 1) * own_count)
            sections.append(shifted(context_packed[rows], -k, ctx_count))
        (block_out,) = attention(q_block, [(anchor, None), (kv_block, "causal")], True)
        (query_out,) = attention(
            query_q,
            [(anchor, None), (all_query_kv, "pos")],
            False,
            positions=(slot_pos, own_pos),
            sections=sections,
        )
        return (block_out, query_out)

    return local


def solution(mesh):
    in_specs = (
        P(("groups", "ctx"), "head"),
        P(None, ("groups", "ctx"), "head"),
        P(None, ("groups", "ctx"), "head"),
        P(None, ("groups", "ctx"), "head"),
        P(("groups", "ctx")),
        P(("groups", "ctx"), "head"),
        P(None, ("groups", "ctx"), "head"),
        P("groups"),
    )
    out_specs = (P(("groups", "ctx"), "head"), P(("groups", "ctx"), "head"))
    return jax.shard_map(
        make_local(mesh.shape["ctx"]),
        mesh=mesh,
        in_specs=in_specs,
        out_specs=out_specs,
        check_vma=False,
    )
```

```python
import functools

import jax
import jax.numpy as jnp
from jax import lax
from jax.experimental import pallas as pl
from jax.experimental.pallas import tpu as pltpu
from jax.sharding import PartitionSpec as P

HD = 128


masked_score = -1e30


def widen(per_head):
    return jnp.repeat(per_head, HD, axis=-1)


STACK_ROWS = 512
CONTEXT_STACK_ROWS = 256


def attention_kernel(
    masks, normalize, packed, rows, group_size, kv_heads, stack_rows, merge_count, *refs
):
    length_ref, q_ref = refs[0], refs[1]
    part_count = len(masks)
    kv_refs = refs[2 : 2 + 2 * part_count]
    rest = refs[2 + 2 * part_count :]
    if "pos" in masks:
        key_pos_ref, own_pos_ref = rest[0], rest[1]
        rest = rest[2:]
    section_refs = rest[: 2 * merge_count]
    rest = rest[2 * merge_count :]
    out_ref = rest[0]
    out_refs = rest[: packed] if packed else None
    side_ref = None if normalize or packed or merge_count else rest[1]
    query_width = kv_heads * group_size * HD
    scale = 1.0 / jnp.sqrt(jnp.float32(HD))
    stack = max(1, min(group_size, stack_rows // rows))
    visible = []
    for index, mask in enumerate(masks):
        key_count = kv_refs[2 * index].shape[0]
        shape = (rows * stack, key_count)
        if mask is None:
            visible.append(None)
        elif mask == "cache":
            cols = lax.broadcasted_iota(jnp.int32, shape, 1)
            visible.append(cols < length_ref[0])
        elif mask == "causal":
            cols = lax.broadcasted_iota(jnp.int32, shape, 1)
            tokens = lax.broadcasted_iota(jnp.int32, shape, 0)
            if stack > 1:
                tokens = lax.rem(tokens, rows)
            visible.append(cols <= tokens)
        else:
            own = own_pos_ref[...]
            if stack > 1:
                own = jnp.concatenate([own] * stack, axis=0)
            visible.append(key_pos_ref[...] <= own)
    for first in range(0, group_size, stack):
        heads = list(range(first, min(group_size, first + stack)))
        if len(heads) == 1:
            lhs = q_ref[:, first * HD : (first + 1) * HD]
        else:
            lhs = jnp.concatenate([q_ref[:, h * HD : (h + 1) * HD] for h in heads], axis=0)
        m_rows = lhs.shape[0]
        all_scores = []
        for index in range(part_count):
            raw = lax.dot_general(
                lhs,
                kv_refs[2 * index][...],
                (((1,), (1,)), ((), ())),
                preferred_element_type=jnp.float32,
            )
            if visible[index] is not None:
                raw = jnp.where(visible[index][:m_rows], raw, -jnp.inf)
            all_scores.append(raw)
        peak = jnp.max(all_scores[0], axis=1, keepdims=True)
        for raw in all_scores[1:]:
            peak = jnp.maximum(peak, jnp.max(raw, axis=1, keepdims=True))
        peak = peak * scale
        total = None
        output = None
        for index, raw in enumerate(all_scores):
            weights = jnp.exp(raw * scale - peak)
            part_total = jnp.sum(weights, axis=1, keepdims=True)
            part_output = jnp.dot(
                weights.astype(jnp.bfloat16),
                kv_refs[2 * index + 1][...],
                preferred_element_type=jnp.float32,
            )
            total = part_total if total is None else total + part_total
            output = part_output if output is None else output + part_output
        for slot, h in enumerate(heads):
            rows_of = slice(slot * rows, (slot + 1) * rows)
            if merge_count:
                peaks = [peak[rows_of]]
                totals = [total[rows_of]]
                outputs = [output[rows_of]]
                for index in range(merge_count):
                    section_o, section_side = section_refs[2 * index], section_refs[2 * index + 1]
                    peaks.append(section_side[:, h : h + 1])
                    totals.append(section_side[:, HD // 2 + h : HD // 2 + h + 1])
                    outputs.append(section_o[:, h * HD : (h + 1) * HD])
                top = peaks[0]
                for value in peaks[1:]:
                    top = jnp.maximum(top, value)
                merged_total = None
                merged_output = None
                for value, part_total, part_output in zip(peaks, totals, outputs):
                    factor = jnp.exp(value - top)
                    t = part_total * factor
                    o = part_output * factor
                    merged_total = t if merged_total is None else merged_total + t
                    merged_output = o if merged_output is None else merged_output + o
                out_ref[:, h * HD : (h + 1) * HD] = (merged_output / merged_total).astype(
                    out_ref.dtype
                )
            elif normalize:
                out_ref[:, h * HD : (h + 1) * HD] = (output[rows_of] / total[rows_of]).astype(
                    out_ref.dtype
                )
            elif packed:

                def store(gi, h=h, rows_of=rows_of):
                    head = gi * group_size + h
                    side = query_width + gi * HD
                    head_output = output[rows_of]
                    head_peak = peak[rows_of]
                    head_total = total[rows_of]
                    own = rows // packed
                    for k, target in enumerate(out_refs):
                        mine = slice(k * own, (k + 1) * own)
                        target[:, head * HD : (head + 1) * HD] = head_output[mine]
                        target[:, side + h : side + h + 1] = head_peak[mine]
                        target[:, side + HD // 2 + h : side + HD // 2 + h + 1] = head_total[mine]

                for gi in range(kv_heads):
                    pl.when(pl.program_id(0) == gi)(functools.partial(store, gi))
            else:
                out_ref[:, h * HD : (h + 1) * HD] = output[rows_of]
                side_ref[:, h : h + 1] = peak[rows_of]
                side_ref[:, HD // 2 + h : HD // 2 + h + 1] = total[rows_of]


def attention(
    queries,
    parts,
    normalize,
    length=None,
    positions=None,
    packed=False,
    stack_rows=STACK_ROWS,
    sections=(),
):
    rows, query_width = queries.shape
    kv_heads = parts[0][0].shape[2] // HD
    group_size = query_width // HD // kv_heads
    group_width = group_size * HD
    if length is None:
        length = jnp.zeros((1,), jnp.int32)
    masks = tuple(mask for _, mask in parts)
    in_specs = [pl.BlockSpec((rows, group_width), lambda g, n: (0, g))]
    operands = [queries]
    for pair, _ in parts:
        key_count = pair.shape[1]
        in_specs.append(pl.BlockSpec((pl.Squeezed(), key_count, HD), lambda g, n: (0, 0, g)))
        in_specs.append(pl.BlockSpec((pl.Squeezed(), key_count, HD), lambda g, n: (1, 0, g)))
        operands += [pair, pair]
    if positions is not None:
        key_pos = positions[0].reshape(1, -1)
        own_pos = positions[1].reshape(-1, 1)
        in_specs.append(pl.BlockSpec(key_pos.shape, lambda g, n: (0, 0)))
        in_specs.append(pl.BlockSpec(own_pos.shape, lambda g, n: (0, 0)))
        operands += [key_pos, own_pos]
    for section in sections:
        side_block = query_width // HD
        in_specs.append(pl.BlockSpec((rows, group_width), lambda g, n: (0, g)))
        in_specs.append(pl.BlockSpec((rows, HD), lambda g, n, c=side_block: (0, c + g)))
        operands += [section, section]
    if sections:
        normalize = True
    out_shape = [
        jax.ShapeDtypeStruct((rows, query_width), jnp.bfloat16 if normalize else jnp.float32)
    ]
    out_specs = [pl.BlockSpec((rows, group_width), lambda g, n: (0, g))]
    if packed:
        full = (rows // packed, query_width + kv_heads * HD)
        out_shape = [jax.ShapeDtypeStruct(full, jnp.float32)] * packed
        out_specs = [pl.BlockSpec(full, lambda g, n: (0, 0))] * packed
    elif not normalize:
        out_shape.append(jax.ShapeDtypeStruct((kv_heads, rows, HD), jnp.float32))
        out_specs.append(pl.BlockSpec((pl.Squeezed(), rows, HD), lambda g, n: (g, 0, 0)))
    return pl.pallas_call(
        functools.partial(
            attention_kernel,
            masks,
            normalize,
            packed,
            rows,
            group_size,
            kv_heads,
            stack_rows,
            len(sections),
        ),
        grid_spec=pltpu.PrefetchScalarGridSpec(
            num_scalar_prefetch=1,
            grid=(kv_heads,),
            in_specs=in_specs,
            out_specs=out_specs,
        ),
        out_shape=out_shape,
    )(length, *operands)


def shifted(value, shift, count):
    return lax.ppermute(value, "ctx", [(j, (j + shift) % count) for j in range(count)])


def make_local(ctx_count):
    def local(q_block, kv_block, anchor_kv, cache_kv, cache_len, query_q, query_kv, query_pos):
        me = lax.axis_index("ctx")
        own_count = query_q.shape[0]
        width = kv_block.shape[2]
        query_width = query_q.shape[1]
        kv_heads = width // HD
        group_size = query_width // HD // kv_heads
        packed = jnp.concatenate([query_q.reshape(-1), query_kv.reshape(-1)])
        query_slots = [packed] + [shifted(packed, k, ctx_count) for k in range(1, ctx_count)]
        anchor_slots = [anchor_kv] + [shifted(anchor_kv, k, ctx_count) for k in range(1, ctx_count)]
        split = own_count * query_width
        all_queries = jnp.concatenate(
            [slot[:split].reshape(own_count, query_width) for slot in query_slots], axis=0
        )
        all_query_kv = jnp.concatenate(
            [slot[split:].reshape(2, own_count, width) for slot in query_slots], axis=1
        )
        anchor = jnp.concatenate(anchor_slots, axis=1)
        slot_pos = jnp.concatenate(
            [
                lax.dynamic_slice_in_dim(query_pos, ((me - k) % ctx_count) * own_count, own_count)
                for k in range(ctx_count)
            ]
        )
        own_pos = slot_pos[:own_count]

        context_slots = attention(
            all_queries,
            [(cache_kv, "cache"), (kv_block, None)],
            False,
            length=cache_len,
            packed=ctx_count,
            stack_rows=CONTEXT_STACK_ROWS,
        )
        sections = [context_slots[0]] + [
            shifted(context_slots[k], -k, ctx_count) for k in range(1, ctx_count)
        ]
        (block_out,) = attention(q_block, [(anchor, None), (kv_block, "causal")], True)
        (query_out,) = attention(
            query_q,
            [(anchor, None), (all_query_kv, "pos")],
            False,
            positions=(slot_pos, own_pos),
            sections=sections,
        )
        return (block_out, query_out)

    return local


def solution(mesh):
    in_specs = (
        P(("groups", "ctx"), "head"),
        P(None, ("groups", "ctx"), "head"),
        P(None, ("groups", "ctx"), "head"),
        P(None, ("groups", "ctx"), "head"),
        P(("groups", "ctx")),
        P(("groups", "ctx"), "head"),
        P(None, ("groups", "ctx"), "head"),
        P("groups"),
    )
    out_specs = (P(("groups", "ctx"), "head"), P(("groups", "ctx"), "head"))
    return jax.shard_map(
        make_local(mesh.shape["ctx"]),
        mesh=mesh,
        in_specs=in_specs,
        out_specs=out_specs,
        check_vma=False,
    )
```

```python
import functools

import jax
import jax.numpy as jnp
from jax import lax
from jax.experimental import pallas as pl
from jax.experimental.pallas import tpu as pltpu
from jax.sharding import PartitionSpec as P

HD = 128


masked_score = -1e30


def widen(per_head):
    return jnp.repeat(per_head, HD, axis=-1)


STACK_ROWS = 512
CONTEXT_STACK_ROWS = 256


def attention_kernel(
    masks, normalize, packed, rows, group_size, kv_heads, stack_rows, merge_count, *refs
):
    length_ref, q_ref = refs[0], refs[1]
    part_count = len(masks)
    kv_refs = refs[2 : 2 + 2 * part_count]
    rest = refs[2 + 2 * part_count :]
    if "pos" in masks:
        key_pos_ref, own_pos_ref = rest[0], rest[1]
        rest = rest[2:]
    section_refs = rest[: 2 * merge_count]
    rest = rest[2 * merge_count :]
    out_ref = rest[0]
    side_ref = None if normalize or packed or merge_count else rest[1]
    query_width = kv_heads * group_size * HD
    scale = 1.0 / jnp.sqrt(jnp.float32(HD))
    stack = max(1, min(group_size, stack_rows // rows))
    visible = []
    for index, mask in enumerate(masks):
        key_count = kv_refs[2 * index].shape[0]
        shape = (rows * stack, key_count)
        if mask is None:
            visible.append(None)
        elif mask == "cache":
            cols = lax.broadcasted_iota(jnp.int32, shape, 1)
            visible.append(cols < length_ref[0])
        elif mask == "causal":
            cols = lax.broadcasted_iota(jnp.int32, shape, 1)
            tokens = lax.broadcasted_iota(jnp.int32, shape, 0)
            if stack > 1:
                tokens = lax.rem(tokens, rows)
            visible.append(cols <= tokens)
        else:
            own = own_pos_ref[...]
            if stack > 1:
                own = jnp.concatenate([own] * stack, axis=0)
            visible.append(key_pos_ref[...] <= own)
    for first in range(0, group_size, stack):
        heads = list(range(first, min(group_size, first + stack)))
        if len(heads) == 1:
            lhs = q_ref[:, first * HD : (first + 1) * HD]
        else:
            lhs = jnp.concatenate([q_ref[:, h * HD : (h + 1) * HD] for h in heads], axis=0)
        m_rows = lhs.shape[0]
        all_scores = []
        for index in range(part_count):
            raw = lax.dot_general(
                lhs,
                kv_refs[2 * index][...],
                (((1,), (1,)), ((), ())),
                preferred_element_type=jnp.float32,
            )
            if visible[index] is not None:
                raw = jnp.where(visible[index][:m_rows], raw, -jnp.inf)
            all_scores.append(raw)
        peak = jnp.max(all_scores[0], axis=1, keepdims=True)
        for raw in all_scores[1:]:
            peak = jnp.maximum(peak, jnp.max(raw, axis=1, keepdims=True))
        peak = peak * scale
        total = None
        output = None
        for index, raw in enumerate(all_scores):
            weights = jnp.exp(raw * scale - peak)
            part_total = jnp.sum(weights, axis=1, keepdims=True)
            part_output = jnp.dot(
                weights.astype(jnp.bfloat16),
                kv_refs[2 * index + 1][...],
                preferred_element_type=jnp.float32,
            )
            total = part_total if total is None else total + part_total
            output = part_output if output is None else output + part_output
        for slot, h in enumerate(heads):
            rows_of = slice(slot * rows, (slot + 1) * rows)
            if merge_count:
                peaks = [peak[rows_of]]
                totals = [total[rows_of]]
                outputs = [output[rows_of]]
                for index in range(merge_count):
                    section_o, section_side = section_refs[2 * index], section_refs[2 * index + 1]
                    peaks.append(section_side[:, h : h + 1])
                    totals.append(section_side[:, HD // 2 + h : HD // 2 + h + 1])
                    outputs.append(section_o[:, h * HD : (h + 1) * HD])
                top = peaks[0]
                for value in peaks[1:]:
                    top = jnp.maximum(top, value)
                merged_total = None
                merged_output = None
                for value, part_total, part_output in zip(peaks, totals, outputs):
                    factor = jnp.exp(value - top)
                    t = part_total * factor
                    o = part_output * factor
                    merged_total = t if merged_total is None else merged_total + t
                    merged_output = o if merged_output is None else merged_output + o
                out_ref[:, h * HD : (h + 1) * HD] = (merged_output / merged_total).astype(
                    out_ref.dtype
                )
            elif normalize:
                out_ref[:, h * HD : (h + 1) * HD] = (output[rows_of] / total[rows_of]).astype(
                    out_ref.dtype
                )
            elif packed:

                def store(gi, h=h, rows_of=rows_of):
                    head = gi * group_size + h
                    out_ref[:, head * HD : (head + 1) * HD] = output[rows_of]
                    side = query_width + gi * HD
                    out_ref[:, side + h : side + h + 1] = peak[rows_of]
                    side += HD // 2
                    out_ref[:, side + h : side + h + 1] = total[rows_of]

                for gi in range(kv_heads):
                    pl.when(pl.program_id(0) == gi)(functools.partial(store, gi))
            else:
                out_ref[:, h * HD : (h + 1) * HD] = output[rows_of]
                side_ref[:, h : h + 1] = peak[rows_of]
                side_ref[:, HD // 2 + h : HD // 2 + h + 1] = total[rows_of]


def attention(
    queries,
    parts,
    normalize,
    length=None,
    positions=None,
    packed=False,
    stack_rows=STACK_ROWS,
    sections=(),
):
    rows, query_width = queries.shape
    kv_heads = parts[0][0].shape[2] // HD
    group_size = query_width // HD // kv_heads
    group_width = group_size * HD
    if length is None:
        length = jnp.zeros((1,), jnp.int32)
    masks = tuple(mask for _, mask in parts)
    in_specs = [pl.BlockSpec((rows, group_width), lambda g, n: (0, g))]
    operands = [queries]
    for pair, _ in parts:
        key_count = pair.shape[1]
        in_specs.append(pl.BlockSpec((pl.Squeezed(), key_count, HD), lambda g, n: (0, 0, g)))
        in_specs.append(pl.BlockSpec((pl.Squeezed(), key_count, HD), lambda g, n: (1, 0, g)))
        operands += [pair, pair]
    if positions is not None:
        key_pos = positions[0].reshape(1, -1)
        own_pos = positions[1].reshape(-1, 1)
        in_specs.append(pl.BlockSpec(key_pos.shape, lambda g, n: (0, 0)))
        in_specs.append(pl.BlockSpec(own_pos.shape, lambda g, n: (0, 0)))
        operands += [key_pos, own_pos]
    for section in sections:
        side_block = query_width // HD
        in_specs.append(pl.BlockSpec((rows, group_width), lambda g, n: (0, g)))
        in_specs.append(pl.BlockSpec((rows, HD), lambda g, n, c=side_block: (0, c + g)))
        operands += [section, section]
    if sections:
        normalize = True
    out_shape = [
        jax.ShapeDtypeStruct((rows, query_width), jnp.bfloat16 if normalize else jnp.float32)
    ]
    out_specs = [pl.BlockSpec((rows, group_width), lambda g, n: (0, g))]
    if packed:
        full = (rows, query_width + kv_heads * HD)
        out_shape = [jax.ShapeDtypeStruct(full, jnp.float32)]
        out_specs = [pl.BlockSpec(full, lambda g, n: (0, 0))]
    elif not normalize:
        out_shape.append(jax.ShapeDtypeStruct((kv_heads, rows, HD), jnp.float32))
        out_specs.append(pl.BlockSpec((pl.Squeezed(), rows, HD), lambda g, n: (g, 0, 0)))
    return pl.pallas_call(
        functools.partial(
            attention_kernel,
            masks,
            normalize,
            packed,
            rows,
            group_size,
            kv_heads,
            stack_rows,
            len(sections),
        ),
        grid_spec=pltpu.PrefetchScalarGridSpec(
            num_scalar_prefetch=1,
            grid=(kv_heads,),
            in_specs=in_specs,
            out_specs=out_specs,
        ),
        out_shape=out_shape,
    )(length, *operands)


def shifted(value, shift, count):
    return lax.ppermute(value, "ctx", [(j, (j + shift) % count) for j in range(count)])


def make_local(ctx_count):
    def local(q_block, kv_block, anchor_kv, cache_kv, cache_len, query_q, query_kv, query_pos):
        me = lax.axis_index("ctx")
        own_count = query_q.shape[0]
        width = kv_block.shape[2]
        query_width = query_q.shape[1]
        kv_heads = width // HD
        group_size = query_width // HD // kv_heads
        packed = jnp.concatenate([query_q.reshape(-1), query_kv.reshape(-1)])
        query_slots = [packed] + [shifted(packed, k, ctx_count) for k in range(1, ctx_count)]
        anchor_slots = [anchor_kv] + [shifted(anchor_kv, k, ctx_count) for k in range(1, ctx_count)]
        split = own_count * query_width
        all_queries = jnp.concatenate(
            [slot[:split].reshape(own_count, query_width) for slot in query_slots], axis=0
        )
        all_query_kv = jnp.concatenate(
            [slot[split:].reshape(2, own_count, width) for slot in query_slots], axis=1
        )
        anchor = jnp.concatenate(anchor_slots, axis=1)
        reversed_pos = query_pos.reshape(ctx_count, own_count)[::-1]
        doubled = jnp.concatenate([reversed_pos, reversed_pos], axis=0)
        slot_pos = lax.dynamic_slice_in_dim(doubled, ctx_count - 1 - me, ctx_count).reshape(-1)
        own_pos = slot_pos[:own_count]

        (context_packed,) = attention(
            all_queries,
            [(cache_kv, "cache"), (kv_block, None)],
            False,
            length=cache_len,
            packed=True,
            stack_rows=CONTEXT_STACK_ROWS,
        )
        sections = [context_packed[:own_count]]
        for k in range(1, ctx_count):
            rows = slice(k * own_count, (k + 1) * own_count)
            sections.append(shifted(context_packed[rows], -k, ctx_count))
        (block_out,) = attention(q_block, [(anchor, None), (kv_block, "causal")], True)
        (query_out,) = attention(
            query_q,
            [(anchor, None), (all_query_kv, "pos")],
            False,
            positions=(slot_pos, own_pos),
            sections=sections,
        )
        return (block_out, query_out)

    return local


def solution(mesh):
    in_specs = (
        P(("groups", "ctx"), "head"),
        P(None, ("groups", "ctx"), "head"),
        P(None, ("groups", "ctx"), "head"),
        P(None, ("groups", "ctx"), "head"),
        P(("groups", "ctx")),
        P(("groups", "ctx"), "head"),
        P(None, ("groups", "ctx"), "head"),
        P("groups"),
    )
    out_specs = (P(("groups", "ctx"), "head"), P(("groups", "ctx"), "head"))
    return jax.shard_map(
        make_local(mesh.shape["ctx"]),
        mesh=mesh,
        in_specs=in_specs,
        out_specs=out_specs,
        check_vma=False,
    )
```

```python
import functools

import jax
import jax.numpy as jnp
from jax import lax
from jax.experimental import pallas as pl
from jax.experimental.pallas import tpu as pltpu
from jax.sharding import PartitionSpec as P

HD = 128


masked_score = -1e30


def widen(per_head):
    return jnp.repeat(per_head, HD, axis=-1)


STACK_ROWS = 768
CONTEXT_STACK_ROWS = 256


def attention_kernel(
    masks, normalize, packed, rows, group_size, kv_heads, stack_rows, merge_count, *refs
):
    length_ref, q_ref = refs[0], refs[1]
    part_count = len(masks)
    kv_refs = refs[2 : 2 + 2 * part_count]
    rest = refs[2 + 2 * part_count :]
    if "pos" in masks:
        key_pos_ref, own_pos_ref = rest[0], rest[1]
        rest = rest[2:]
    section_refs = rest[: 2 * merge_count]
    rest = rest[2 * merge_count :]
    out_ref = rest[0]
    side_ref = None if normalize or packed or merge_count else rest[1]
    query_width = kv_heads * group_size * HD
    scale = 1.0 / jnp.sqrt(jnp.float32(HD))
    stack = max(1, min(group_size, stack_rows // rows))
    visible = []
    for index, mask in enumerate(masks):
        key_count = kv_refs[2 * index].shape[0]
        shape = (rows * stack, key_count)
        if mask is None:
            visible.append(None)
        elif mask == "cache":
            cols = lax.broadcasted_iota(jnp.int32, shape, 1)
            visible.append(cols < length_ref[0])
        elif mask == "causal":
            cols = lax.broadcasted_iota(jnp.int32, shape, 1)
            tokens = lax.broadcasted_iota(jnp.int32, shape, 0)
            if stack > 1:
                tokens = lax.rem(tokens, rows)
            visible.append(cols <= tokens)
        else:
            own = own_pos_ref[...]
            if stack > 1:
                own = jnp.concatenate([own] * stack, axis=0)
            visible.append(key_pos_ref[...] <= own)
    for first in range(0, group_size, stack):
        heads = list(range(first, min(group_size, first + stack)))
        if len(heads) == 1:
            lhs = q_ref[:, first * HD : (first + 1) * HD]
        else:
            lhs = jnp.concatenate([q_ref[:, h * HD : (h + 1) * HD] for h in heads], axis=0)
        m_rows = lhs.shape[0]
        all_scores = []
        for index in range(part_count):
            raw = lax.dot_general(
                lhs,
                kv_refs[2 * index][...],
                (((1,), (1,)), ((), ())),
                preferred_element_type=jnp.float32,
            )
            if visible[index] is not None:
                raw = jnp.where(visible[index][:m_rows], raw, -jnp.inf)
            all_scores.append(raw)
        peak = jnp.max(all_scores[0], axis=1, keepdims=True)
        for raw in all_scores[1:]:
            peak = jnp.maximum(peak, jnp.max(raw, axis=1, keepdims=True))
        peak = peak * scale
        total = None
        output = None
        for index, raw in enumerate(all_scores):
            weights = jnp.exp(raw * scale - peak)
            part_total = jnp.sum(weights, axis=1, keepdims=True)
            part_output = jnp.dot(
                weights.astype(jnp.bfloat16),
                kv_refs[2 * index + 1][...],
                preferred_element_type=jnp.float32,
            )
            total = part_total if total is None else total + part_total
            output = part_output if output is None else output + part_output
        for slot, h in enumerate(heads):
            rows_of = slice(slot * rows, (slot + 1) * rows)
            if merge_count:
                peaks = [peak[rows_of]]
                totals = [total[rows_of]]
                outputs = [output[rows_of]]
                for index in range(merge_count):
                    section_o, section_side = section_refs[2 * index], section_refs[2 * index + 1]
                    peaks.append(section_side[:, h : h + 1])
                    totals.append(section_side[:, HD // 2 + h : HD // 2 + h + 1])
                    outputs.append(section_o[:, h * HD : (h + 1) * HD])
                top = peaks[0]
                for value in peaks[1:]:
                    top = jnp.maximum(top, value)
                merged_total = None
                merged_output = None
                for value, part_total, part_output in zip(peaks, totals, outputs):
                    factor = jnp.exp(value - top)
                    t = part_total * factor
                    o = part_output * factor
                    merged_total = t if merged_total is None else merged_total + t
                    merged_output = o if merged_output is None else merged_output + o
                out_ref[:, h * HD : (h + 1) * HD] = (merged_output / merged_total).astype(
                    out_ref.dtype
                )
            elif normalize:
                out_ref[:, h * HD : (h + 1) * HD] = (output[rows_of] / total[rows_of]).astype(
                    out_ref.dtype
                )
            elif packed:

                def store(gi, h=h, rows_of=rows_of):
                    head = gi * group_size + h
                    out_ref[:, head * HD : (head + 1) * HD] = output[rows_of]
                    side = query_width + gi * HD
                    out_ref[:, side + h : side + h + 1] = peak[rows_of]
                    side += HD // 2
                    out_ref[:, side + h : side + h + 1] = total[rows_of]

                for gi in range(kv_heads):
                    pl.when(pl.program_id(0) == gi)(functools.partial(store, gi))
            else:
                out_ref[:, h * HD : (h + 1) * HD] = output[rows_of]
                side_ref[:, h : h + 1] = peak[rows_of]
                side_ref[:, HD // 2 + h : HD // 2 + h + 1] = total[rows_of]


def attention(
    queries,
    parts,
    normalize,
    length=None,
    positions=None,
    packed=False,
    stack_rows=STACK_ROWS,
    sections=(),
):
    rows, query_width = queries.shape
    kv_heads = parts[0][0].shape[2] // HD
    group_size = query_width // HD // kv_heads
    group_width = group_size * HD
    if length is None:
        length = jnp.zeros((1,), jnp.int32)
    masks = tuple(mask for _, mask in parts)
    in_specs = [pl.BlockSpec((rows, group_width), lambda g, n: (0, g))]
    operands = [queries]
    for pair, _ in parts:
        key_count = pair.shape[1]
        in_specs.append(pl.BlockSpec((pl.Squeezed(), key_count, HD), lambda g, n: (0, 0, g)))
        in_specs.append(pl.BlockSpec((pl.Squeezed(), key_count, HD), lambda g, n: (1, 0, g)))
        operands += [pair, pair]
    if positions is not None:
        key_pos = positions[0].reshape(1, -1)
        own_pos = positions[1].reshape(-1, 1)
        in_specs.append(pl.BlockSpec(key_pos.shape, lambda g, n: (0, 0)))
        in_specs.append(pl.BlockSpec(own_pos.shape, lambda g, n: (0, 0)))
        operands += [key_pos, own_pos]
    for section in sections:
        side_block = query_width // HD
        in_specs.append(pl.BlockSpec((rows, group_width), lambda g, n: (0, g)))
        in_specs.append(pl.BlockSpec((rows, HD), lambda g, n, c=side_block: (0, c + g)))
        operands += [section, section]
    if sections:
        normalize = True
    out_shape = [
        jax.ShapeDtypeStruct((rows, query_width), jnp.bfloat16 if normalize else jnp.float32)
    ]
    out_specs = [pl.BlockSpec((rows, group_width), lambda g, n: (0, g))]
    if packed:
        full = (rows, query_width + kv_heads * HD)
        out_shape = [jax.ShapeDtypeStruct(full, jnp.float32)]
        out_specs = [pl.BlockSpec(full, lambda g, n: (0, 0))]
    elif not normalize:
        out_shape.append(jax.ShapeDtypeStruct((kv_heads, rows, HD), jnp.float32))
        out_specs.append(pl.BlockSpec((pl.Squeezed(), rows, HD), lambda g, n: (g, 0, 0)))
    return pl.pallas_call(
        functools.partial(
            attention_kernel,
            masks,
            normalize,
            packed,
            rows,
            group_size,
            kv_heads,
            stack_rows,
            len(sections),
        ),
        grid_spec=pltpu.PrefetchScalarGridSpec(
            num_scalar_prefetch=1,
            grid=(kv_heads,),
            in_specs=in_specs,
            out_specs=out_specs,
        ),
        out_shape=out_shape,
    )(length, *operands)


def shifted(value, shift, count):
    return lax.ppermute(value, "ctx", [(j, (j + shift) % count) for j in range(count)])


def make_local(ctx_count):
    def local(q_block, kv_block, anchor_kv, cache_kv, cache_len, query_q, query_kv, query_pos):
        me = lax.axis_index("ctx")
        own_count = query_q.shape[0]
        width = kv_block.shape[2]
        query_width = query_q.shape[1]
        kv_heads = width // HD
        group_size = query_width // HD // kv_heads
        packed = jnp.concatenate([query_q.reshape(-1), query_kv.reshape(-1)])
        query_slots = [packed] + [shifted(packed, k, ctx_count) for k in range(1, ctx_count)]
        anchor_slots = [anchor_kv] + [shifted(anchor_kv, k, ctx_count) for k in range(1, ctx_count)]
        split = own_count * query_width
        all_queries = jnp.concatenate(
            [slot[:split].reshape(own_count, query_width) for slot in query_slots], axis=0
        )
        all_query_kv = jnp.concatenate(
            [slot[split:].reshape(2, own_count, width) for slot in query_slots], axis=1
        )
        anchor = jnp.concatenate(anchor_slots, axis=1)
        slot_pos = jnp.concatenate(
            [
                lax.dynamic_slice_in_dim(query_pos, ((me - k) % ctx_count) * own_count, own_count)
                for k in range(ctx_count)
            ]
        )
        own_pos = slot_pos[:own_count]

        (context_packed,) = attention(
            all_queries,
            [(cache_kv, "cache"), (kv_block, None)],
            False,
            length=cache_len,
            packed=True,
            stack_rows=CONTEXT_STACK_ROWS,
        )
        sections = [context_packed[:own_count]]
        for k in range(1, ctx_count):
            rows = slice(k * own_count, (k + 1) * own_count)
            sections.append(shifted(context_packed[rows], -k, ctx_count))
        (block_out,) = attention(q_block, [(anchor, None), (kv_block, "causal")], True)
        (query_out,) = attention(
            query_q,
            [(anchor, None), (all_query_kv, "pos")],
            False,
            positions=(slot_pos, own_pos),
            sections=sections,
        )
        return (block_out, query_out)

    return local


def solution(mesh):
    in_specs = (
        P(("groups", "ctx"), "head"),
        P(None, ("groups", "ctx"), "head"),
        P(None, ("groups", "ctx"), "head"),
        P(None, ("groups", "ctx"), "head"),
        P(("groups", "ctx")),
        P(("groups", "ctx"), "head"),
        P(None, ("groups", "ctx"), "head"),
        P("groups"),
    )
    out_specs = (P(("groups", "ctx"), "head"), P(("groups", "ctx"), "head"))
    return jax.shard_map(
        make_local(mesh.shape["ctx"]),
        mesh=mesh,
        in_specs=in_specs,
        out_specs=out_specs,
        check_vma=False,
    )
```

```python
import functools

import jax
import jax.numpy as jnp
from jax import lax
from jax.experimental import pallas as pl
from jax.experimental.pallas import tpu as pltpu
from jax.sharding import PartitionSpec as P

HD = 128


masked_score = -1e30


def widen(per_head):
    return jnp.repeat(per_head, HD, axis=-1)


STACK_ROWS = 768
CONTEXT_STACK_ROWS = 256


def attention_kernel(
    masks, normalize, packed, rows, group_size, kv_heads, stack_rows, merge_count, *refs
):
    length_ref, q_ref = refs[0], refs[1]
    part_count = len(masks)
    kv_refs = refs[2 : 2 + 2 * part_count]
    rest = refs[2 + 2 * part_count :]
    if "pos" in masks:
        key_pos_ref, own_pos_ref = rest[0], rest[1]
        rest = rest[2:]
    section_refs = rest[: 2 * merge_count]
    rest = rest[2 * merge_count :]
    out_ref = rest[0]
    side_ref = None if normalize or packed or merge_count else rest[1]
    query_width = kv_heads * group_size * HD
    scale = 1.0 / jnp.sqrt(jnp.float32(HD))
    stack = max(1, min(group_size, stack_rows // rows))
    visible = []
    for index, mask in enumerate(masks):
        key_count = kv_refs[2 * index].shape[0]
        shape = (rows * stack, key_count)
        if mask is None:
            visible.append(None)
        elif mask == "cache":
            cols = lax.broadcasted_iota(jnp.int32, shape, 1)
            visible.append(cols < length_ref[0])
        elif mask == "causal":
            cols = lax.broadcasted_iota(jnp.int32, (rows, key_count), 1)
            tokens = lax.broadcasted_iota(jnp.int32, (rows, key_count), 0)
            causal = cols <= tokens
            if stack > 1:
                causal = jnp.concatenate([causal] * stack, axis=0)
            visible.append(causal)
        else:
            own = own_pos_ref[...]
            if stack > 1:
                own = jnp.concatenate([own] * stack, axis=0)
            visible.append(key_pos_ref[...] <= own)
    for first in range(0, group_size, stack):
        heads = list(range(first, min(group_size, first + stack)))
        if len(heads) == 1:
            lhs = q_ref[:, first * HD : (first + 1) * HD]
        else:
            lhs = jnp.concatenate([q_ref[:, h * HD : (h + 1) * HD] for h in heads], axis=0)
        m_rows = lhs.shape[0]
        all_scores = []
        for index in range(part_count):
            raw = lax.dot_general(
                lhs,
                kv_refs[2 * index][...],
                (((1,), (1,)), ((), ())),
                preferred_element_type=jnp.float32,
            )
            if visible[index] is not None:
                raw = jnp.where(visible[index][:m_rows], raw, -jnp.inf)
            all_scores.append(raw)
        peak = jnp.max(all_scores[0], axis=1, keepdims=True)
        for raw in all_scores[1:]:
            peak = jnp.maximum(peak, jnp.max(raw, axis=1, keepdims=True))
        peak = peak * scale
        total = None
        output = None
        for index, raw in enumerate(all_scores):
            weights = jnp.exp(raw * scale - peak)
            part_total = jnp.sum(weights, axis=1, keepdims=True)
            part_output = jnp.dot(
                weights.astype(jnp.bfloat16),
                kv_refs[2 * index + 1][...],
                preferred_element_type=jnp.float32,
            )
            total = part_total if total is None else total + part_total
            output = part_output if output is None else output + part_output
        for slot, h in enumerate(heads):
            rows_of = slice(slot * rows, (slot + 1) * rows)
            if merge_count:
                peaks = [peak[rows_of]]
                totals = [total[rows_of]]
                outputs = [output[rows_of]]
                for index in range(merge_count):
                    section_o, section_side = section_refs[2 * index], section_refs[2 * index + 1]
                    peaks.append(section_side[:, h : h + 1])
                    totals.append(section_side[:, HD // 2 + h : HD // 2 + h + 1])
                    outputs.append(section_o[:, h * HD : (h + 1) * HD])
                top = peaks[0]
                for value in peaks[1:]:
                    top = jnp.maximum(top, value)
                merged_total = None
                merged_output = None
                for value, part_total, part_output in zip(peaks, totals, outputs):
                    factor = jnp.exp(value - top)
                    t = part_total * factor
                    o = part_output * factor
                    merged_total = t if merged_total is None else merged_total + t
                    merged_output = o if merged_output is None else merged_output + o
                out_ref[:, h * HD : (h + 1) * HD] = (merged_output / merged_total).astype(
                    out_ref.dtype
                )
            elif normalize:
                out_ref[:, h * HD : (h + 1) * HD] = (output[rows_of] / total[rows_of]).astype(
                    out_ref.dtype
                )
            elif packed:

                def store(gi, h=h, rows_of=rows_of):
                    head = gi * group_size + h
                    out_ref[:, head * HD : (head + 1) * HD] = output[rows_of]
                    side = query_width + gi * HD
                    out_ref[:, side + h : side + h + 1] = peak[rows_of]
                    side += HD // 2
                    out_ref[:, side + h : side + h + 1] = total[rows_of]

                for gi in range(kv_heads):
                    pl.when(pl.program_id(0) == gi)(functools.partial(store, gi))
            else:
                out_ref[:, h * HD : (h + 1) * HD] = output[rows_of]
                side_ref[:, h : h + 1] = peak[rows_of]
                side_ref[:, HD // 2 + h : HD // 2 + h + 1] = total[rows_of]


def attention(
    queries,
    parts,
    normalize,
    length=None,
    positions=None,
    packed=False,
    stack_rows=STACK_ROWS,
    sections=(),
):
    rows, query_width = queries.shape
    kv_heads = parts[0][0].shape[2] // HD
    group_size = query_width // HD // kv_heads
    group_width = group_size * HD
    if length is None:
        length = jnp.zeros((1,), jnp.int32)
    masks = tuple(mask for _, mask in parts)
    in_specs = [pl.BlockSpec((rows, group_width), lambda g, n: (0, g))]
    operands = [queries]
    for pair, _ in parts:
        key_count = pair.shape[1]
        in_specs.append(pl.BlockSpec((pl.Squeezed(), key_count, HD), lambda g, n: (0, 0, g)))
        in_specs.append(pl.BlockSpec((pl.Squeezed(), key_count, HD), lambda g, n: (1, 0, g)))
        operands += [pair, pair]
    if positions is not None:
        key_pos = positions[0].reshape(1, -1)
        own_pos = positions[1].reshape(-1, 1)
        in_specs.append(pl.BlockSpec(key_pos.shape, lambda g, n: (0, 0)))
        in_specs.append(pl.BlockSpec(own_pos.shape, lambda g, n: (0, 0)))
        operands += [key_pos, own_pos]
    for section in sections:
        side_block = query_width // HD
        in_specs.append(pl.BlockSpec((rows, group_width), lambda g, n: (0, g)))
        in_specs.append(pl.BlockSpec((rows, HD), lambda g, n, c=side_block: (0, c + g)))
        operands += [section, section]
    if sections:
        normalize = True
    out_shape = [
        jax.ShapeDtypeStruct((rows, query_width), jnp.bfloat16 if normalize else jnp.float32)
    ]
    out_specs = [pl.BlockSpec((rows, group_width), lambda g, n: (0, g))]
    if packed:
        full = (rows, query_width + kv_heads * HD)
        out_shape = [jax.ShapeDtypeStruct(full, jnp.float32)]
        out_specs = [pl.BlockSpec(full, lambda g, n: (0, 0))]
    elif not normalize:
        out_shape.append(jax.ShapeDtypeStruct((kv_heads, rows, HD), jnp.float32))
        out_specs.append(pl.BlockSpec((pl.Squeezed(), rows, HD), lambda g, n: (g, 0, 0)))
    return pl.pallas_call(
        functools.partial(
            attention_kernel,
            masks,
            normalize,
            packed,
            rows,
            group_size,
            kv_heads,
            stack_rows,
            len(sections),
        ),
        grid_spec=pltpu.PrefetchScalarGridSpec(
            num_scalar_prefetch=1,
            grid=(kv_heads,),
            in_specs=in_specs,
            out_specs=out_specs,
        ),
        out_shape=out_shape,
    )(length, *operands)


def shifted(value, shift, count):
    return lax.ppermute(value, "ctx", [(j, (j + shift) % count) for j in range(count)])


def make_local(ctx_count):
    def local(q_block, kv_block, anchor_kv, cache_kv, cache_len, query_q, query_kv, query_pos):
        me = lax.axis_index("ctx")
        own_count = query_q.shape[0]
        width = kv_block.shape[2]
        query_width = query_q.shape[1]
        kv_heads = width // HD
        group_size = query_width // HD // kv_heads
        packed = jnp.concatenate([query_q.reshape(-1), query_kv.reshape(-1)])
        query_slots = [packed] + [shifted(packed, k, ctx_count) for k in range(1, ctx_count)]
        anchor_slots = [anchor_kv] + [shifted(anchor_kv, k, ctx_count) for k in range(1, ctx_count)]
        split = own_count * query_width
        all_queries = jnp.concatenate(
            [slot[:split].reshape(own_count, query_width) for slot in query_slots], axis=0
        )
        all_query_kv = jnp.concatenate(
            [slot[split:].reshape(2, own_count, width) for slot in query_slots], axis=1
        )
        anchor = jnp.concatenate(anchor_slots, axis=1)
        slot_pos = jnp.concatenate(
            [
                lax.dynamic_slice_in_dim(query_pos, ((me - k) % ctx_count) * own_count, own_count)
                for k in range(ctx_count)
            ]
        )
        own_pos = slot_pos[:own_count]

        (context_packed,) = attention(
            all_queries,
            [(cache_kv, "cache"), (kv_block, None)],
            False,
            length=cache_len,
            packed=True,
            stack_rows=CONTEXT_STACK_ROWS,
        )
        sections = [context_packed[:own_count]]
        for k in range(1, ctx_count):
            rows = slice(k * own_count, (k + 1) * own_count)
            sections.append(shifted(context_packed[rows], -k, ctx_count))
        (block_out,) = attention(q_block, [(anchor, None), (kv_block, "causal")], True)
        (query_out,) = attention(
            query_q,
            [(anchor, None), (all_query_kv, "pos")],
            False,
            positions=(slot_pos, own_pos),
            sections=sections,
        )
        return (block_out, query_out)

    return local


def solution(mesh):
    in_specs = (
        P(("groups", "ctx"), "head"),
        P(None, ("groups", "ctx"), "head"),
        P(None, ("groups", "ctx"), "head"),
        P(None, ("groups", "ctx"), "head"),
        P(("groups", "ctx")),
        P(("groups", "ctx"), "head"),
        P(None, ("groups", "ctx"), "head"),
        P("groups"),
    )
    out_specs = (P(("groups", "ctx"), "head"), P(("groups", "ctx"), "head"))
    return jax.shard_map(
        make_local(mesh.shape["ctx"]),
        mesh=mesh,
        in_specs=in_specs,
        out_specs=out_specs,
        check_vma=False,
    )
```
